256 devices in a mesh: mom: 64 (over x, y, z_lo, core), spin: 4 (over z_hi).
Axes of the slice: x: 4, y: 4, z: 8 (z_hi: 4, z_lo: 2; z = z_hi * 2 + z_lo), core: 2. Of those that a mesh axis runs over, the one named last changes fastest.
Arguments:
- vertex_start: bfloat16 [64, 4, 768, 768], P('mom', 'spin'), may hold values from -6 to 6
- bare_vertex: bfloat16 [64, 4, 768, 768], P('mom', 'spin'), may hold values from -6 to 6
- bubble: bfloat16 [64, 4, 64, 12, 12], P('mom', 'spin'), may hold values from -0.011962891 to 0.011962891
- form_mix: bfloat16 [2, 12, 12], replicated, may hold values from -0.59765625 to 0.59765625
- cross_tables: int32 [2, 64, 64], replicated, may hold values from 0 to 63, as said below
- freq_perm: int32 [2, 64], replicated, may hold values from 0 to 63, each once within a row
Outputs:
- vertex_final: bfloat16 [64, 4, 768, 768], P('mom', 'spin')
The draws below stay inside these ranges and needn't reach their ends.
Inputs may be any that keep to these rules, and one draw needn't show every extreme that they name: `cross_tables`: for each crossing and frequency, the entries over the 64 momenta are a permutation of the momenta; for each crossing and momentum, every momentum appears exactly once over the 64 frequencies.
All inputs are finite; a program needn't handle non-finite values.
Results may differ from the reference program's by a relative error of at most 0.0085.
Values may be sent and summed in bfloat16 or wider, within the bound.
No kernel may reach another device: no remote copies, remote signals or barrier semaphores. Data moves between devices by JAX's collectives and lax.ppermute only.
A program may use at most 64 MiB of HBM per device.

```python
import jax
import jax.numpy as jnp
from jax import lax

NF = 64
FF = 12
ORDER = 768
NQ = 64
NCH = 4
NCROSS = 2
OUTER = 1
INNER = 2


def draw_cross_tables(key, part):
    tables_list = []
    for crossing in range(NCROSS):
        first_key, second_key = jax.random.split(jax.random.fold_in(key, 17 + crossing))
        relabel = jax.random.permutation(first_key, NQ).astype(jnp.int32)
        offsets = jax.random.permutation(second_key, NF).astype(jnp.int32) % NQ
        momenta = jnp.arange(NQ, dtype=jnp.int32)[:, None]
        if crossing % 2 == 0:
            shifted = (offsets[None, :] - momenta) % NQ
        else:
            shifted = (momenta - offsets[None, :]) % NQ
        tables_list.append(relabel[shifted])
    return jnp.stack(tables_list).astype(jnp.int32)


def block_scale(key, dims, cuts, smallest, largest):
    gain = 1.0
    for position, shards_of in cuts:
        heights = jax.random.uniform(jax.random.fold_in(jax.random.fold_in(key, 6), position), (shards_of,), jnp.float32, smallest / len(cuts), largest / len(cuts))
        gain = gain * jnp.repeat(jnp.exp(heights), dims[position] // shards_of).reshape((-1,) + (1,) * (len(dims) - 1 - position))
    return gain


def bell_draw(own_key, extent, width, reach, cuts=(), held_as=jnp.bfloat16):
    drawn = width * jax.random.normal(own_key, extent, jnp.float32)
    if cuts:
        drawn = drawn * block_scale(own_key, extent, cuts, -0.22, 0.18)
    return jnp.clip(drawn, -reach, reach).astype(held_as)


def setup_inputs(seed: int = 0) -> dict:
    arg_keys = jax.random.split(jax.random.key(seed), 7)
    vertex_start = bell_draw(arg_keys[0], (NQ, NCH, ORDER, ORDER), 1.0, 6.0, ((0, 64), (1, 4)))
    bare_vertex = bell_draw(arg_keys[1], (NQ, NCH, ORDER, ORDER), 1.0, 6.0, ((0, 64), (1, 4)))
    bubble = bell_draw(arg_keys[2], (NQ, NCH, NF, FF, FF), 0.002, 0.011962891, ((0, 64), (1, 4)))
    form_mix = bell_draw(arg_keys[3], (NCROSS, FF, FF), 0.1, 0.59765625)
    cross_tables = draw_cross_tables(jax.random.fold_in(arg_keys[6], 71), 0)
    freq_perm = jax.vmap(lambda own: jax.random.permutation(own, NF))(jax.random.split(arg_keys[5], NCROSS)).reshape((NCROSS, NF)).astype(jnp.int32)
    return dict(vertex_start=vertex_start, bare_vertex=bare_vertex, bubble=bubble, form_mix=form_mix, cross_tables=cross_tables, freq_perm=freq_perm)


COEF_SELF = (-0.5, 0.5, 0.5, 0.5)
COEF_PAIR = (-1.5, -0.5, 1.5, -0.5)


def cross_blocks(blocked, table, frequency_perm, mixing):
    mom_index = jnp.broadcast_to(jnp.arange(NQ, dtype=jnp.int32)[:, None], (NQ, NF))
    freq_index = jnp.broadcast_to(jnp.arange(NF, dtype=jnp.int32)[None, :], (NQ, NF))
    inverse = jnp.zeros((NQ, NF), jnp.int32).at[table, freq_index].set(mom_index)
    freq_of = jnp.argsort(frequency_perm).astype(jnp.int32)
    source = inverse[:, freq_of]
    chan_index = jnp.arange(NCH, dtype=jnp.int32)
    gathered = blocked[source[:, None, :], chan_index[None, :, None], freq_of[None, None, :]]
    mixed = jnp.einsum("lm,qcfmb->qcflb", mixing.astype(jnp.float32), gathered.astype(jnp.float32))
    return mixed.reshape(NQ, NCH, ORDER, ORDER)


def inner_solve(items):
    bare_mat, reduced_mat, bubble_mat, current = items
    base_sum = bare_mat.astype(jnp.float32) + reduced_mat.astype(jnp.float32)
    for inner_step in range(INNER):
        carried = jnp.einsum("fln,fnb->flb", bubble_mat.astype(jnp.float32),
                             current.reshape(NF, FF, ORDER).astype(jnp.float32))
        carried = carried.reshape(ORDER, ORDER).astype(jnp.bfloat16)
        total = base_sum + jnp.dot(bare_mat, carried, preferred_element_type=jnp.float32)
        total = total + jnp.dot(reduced_mat, carried, preferred_element_type=jnp.float32)
        current = total.astype(jnp.bfloat16)
    return current


def reference(vertex_start, bare_vertex, bubble, form_mix, cross_tables, freq_perm):
    current = vertex_start
    coef_self = jnp.array(COEF_SELF, jnp.float32)[None, :, None, None]
    coef_pair = jnp.array(COEF_PAIR, jnp.float32)[None, :, None, None]
    partner_index = jnp.array([1, 0, 3, 2], jnp.int32)
    for outer_step in range(OUTER):
        blocked = current.reshape(NQ, NCH, NF, FF, ORDER)
        summed = jnp.zeros((NQ, NCH, ORDER, ORDER), jnp.float32)
        for crossing in range(NCROSS):
            summed = summed + cross_blocks(blocked, cross_tables[crossing], freq_perm[crossing], form_mix[crossing])
        summed = summed.astype(jnp.bfloat16).astype(jnp.float32)
        reducible = (coef_self * summed + coef_pair * summed[:, partner_index]).astype(jnp.bfloat16)
        items = (bare_vertex.reshape(NQ * NCH, ORDER, ORDER), reducible.reshape(NQ * NCH, ORDER, ORDER),
                 bubble.reshape(NQ * NCH, NF, FF, FF), current.reshape(NQ * NCH, ORDER, ORDER))
        current = lax.map(inner_solve, items).reshape(NQ, NCH, ORDER, ORDER)
    return current
```

```python
import jax
import jax.numpy as jnp
from jax import lax
from jax.sharding import PartitionSpec as P

INNER = 2
NCHUNK = 3

COEF_SELF = (-0.5, 0.5, 0.5, 0.5)
COEF_PAIR = (-1.5, -0.5, 1.5, -0.5)


def partner_2(value, axis, stride):
    mask = 2**stride
    pairs = [(source, source ^ mask) for source in range(lax.axis_size(axis))]
    return lax.ppermute(value, axis, pairs)


def inverse_perm(perm, size):
    idx = jnp.arange(size, dtype=jnp.int32)
    return jnp.sum(jnp.where(perm[None, :] == idx[:, None], idx[None, :], 0), axis=1)


def crossing_plan(table, frequency_perm, momentum, freqs):
    idx = jnp.arange(freqs, dtype=jnp.int32)
    own_row = jnp.take(table, momentum, axis=0)
    send_order = inverse_perm(own_row, freqs)
    hit = table == momentum
    source = jnp.sum(jnp.where(hit, idx[:, None], 0), axis=0)
    freq_of = inverse_perm(frequency_perm, freqs)
    return send_order, jnp.take(source, freq_of, axis=0)


def mix_matrix(slots, mixing, freqs):
    forms = mixing.shape[0]
    idx = jnp.arange(freqs, dtype=jnp.int32)
    onehot = (slots[:, None] == idx[None, :]).astype(mixing.dtype)
    full = onehot[:, None, :, None] * mixing[None, :, None, :]
    return full.reshape(freqs * forms, freqs * forms)


def local(vertex_start, bare_vertex, bubble, form_mix, cross_tables, freq_perm):
    current = vertex_start[0, 0]
    bare_mat = bare_vertex[0, 0]
    bubble_mat = bubble[0, 0]
    freqs, forms = (bubble_mat.shape[0], bubble_mat.shape[1])
    order_len = current.shape[0]
    momenta = lax.axis_size("mom")
    assert freqs == momenta
    momentum = lax.axis_index("mom")
    channel = lax.axis_index("spin")
    coef_self = jnp.take(jnp.array(COEF_SELF, jnp.float32), channel)
    coef_pair = jnp.take(jnp.array(COEF_PAIR, jnp.float32), channel)

    blocks = current.reshape(freqs, forms, order_len)
    packs = []
    mixes = []
    for r in range(2):
        send_order, recv_slots = crossing_plan(cross_tables[r], freq_perm[r], momentum, freqs)
        packs.append(jnp.take(blocks, send_order, axis=0))
        mixes.append(mix_matrix(recv_slots, form_mix[r], freqs))
    stacked = jnp.stack(packs)
    mix = jnp.concatenate(mixes, axis=1)

    def carry_of(mat):
        carried = jnp.einsum(
            "fln,fnb->flb",
            bubble_mat,
            mat.reshape(freqs, forms, order_len),
            preferred_element_type=jnp.float32,
        )
        return carried.reshape(order_len, order_len).astype(jnp.bfloat16)

    carried = carry_of(current)
    bare_part = jnp.dot(bare_mat, carried, preferred_element_type=jnp.float32)

    width = order_len // NCHUNK
    red_chunks = []
    for k in range(NCHUNK):
        cols = slice(k * width, (k + 1) * width)
        received = lax.all_to_all(stacked[..., cols], "mom", split_axis=1, concat_axis=1, tiled=True)
        summed = jnp.dot(
            mix, received.reshape(2 * order_len, width), preferred_element_type=jnp.float32
        ).astype(jnp.bfloat16)
        other = partner_2(summed, "spin", 0)
        red_chunks.append(
            (coef_self * summed.astype(jnp.float32) + coef_pair * other.astype(jnp.float32)).astype(
                jnp.bfloat16
            )
        )
    reducible = jnp.concatenate(red_chunks, axis=1)
    base_sum = bare_mat.astype(jnp.float32) + reducible.astype(jnp.float32)

    total = base_sum + bare_part
    for k in range(NCHUNK):
        rows = slice(k * width, (k + 1) * width)
        total = total + jnp.dot(red_chunks[k], carried[rows], preferred_element_type=jnp.float32)
    current = total.astype(jnp.bfloat16)
    for inner_step in range(1, INNER):
        carried = carry_of(current)
        total = base_sum + jnp.dot(bare_mat, carried, preferred_element_type=jnp.float32)
        total = total + jnp.dot(reducible, carried, preferred_element_type=jnp.float32)
        current = total.astype(jnp.bfloat16)
    return current[None, None]


def solution(mesh):
    in_specs = (
        P("mom", "spin", None, None),
        P("mom", "spin", None, None),
        P("mom", "spin", None, None, None),
        P(),
        P(),
        P(),
    )
    out_specs = P("mom", "spin", None, None)
    return jax.shard_map(local, mesh=mesh, in_specs=in_specs, out_specs=out_specs, check_vma=False)
```

```python
import jax
import jax.numpy as jnp
from jax import lax
from jax.sharding import PartitionSpec as P

INNER = 2
NCHUNK = 2

COEF_SELF = (-0.5, 0.5, 0.5, 0.5)
COEF_PAIR = (-1.5, -0.5, 1.5, -0.5)


def partner_2(value, axis, stride):
    mask = 2**stride
    pairs = [(source, source ^ mask) for source in range(lax.axis_size(axis))]
    return lax.ppermute(value, axis, pairs)


def inverse_perm(perm, size):
    idx = jnp.arange(size, dtype=jnp.int32)
    return jnp.sum(jnp.where(perm[None, :] == idx[:, None], idx[None, :], 0), axis=1)


def crossing_plan(table, frequency_perm, momentum, freqs):
    idx = jnp.arange(freqs, dtype=jnp.int32)
    own_row = jnp.take(table, momentum, axis=0)
    send_order = inverse_perm(own_row, freqs)
    hit = table == momentum
    source = jnp.sum(jnp.where(hit, idx[:, None], 0), axis=0)
    freq_of = inverse_perm(frequency_perm, freqs)
    return send_order, jnp.take(source, freq_of, axis=0)


def block_rows(order_len, freqs):
    forms = order_len // freqs
    rows = lax.broadcasted_iota(jnp.int32, (order_len, freqs), 0) // forms
    cols = lax.broadcasted_iota(jnp.int32, (order_len, freqs), 1)
    return (rows == cols).astype(jnp.bfloat16)


def form_rows(order_len, forms):
    rows = lax.broadcasted_iota(jnp.int32, (order_len, forms), 0) % forms
    cols = lax.broadcasted_iota(jnp.int32, (order_len, forms), 1)
    return (rows == cols).astype(jnp.bfloat16)


def exact_dot(a, b):
    return jnp.dot(a, b, preferred_element_type=jnp.float32).astype(jnp.bfloat16)


def mix_matrix(slots, mixing, freqs, expand, forms_expand):
    idx = jnp.arange(freqs, dtype=jnp.int32)
    onehot = (slots[:, None] == idx[None, :]).astype(jnp.bfloat16)
    select = exact_dot(exact_dot(expand, onehot), expand.T)
    tiled = exact_dot(exact_dot(forms_expand, mixing), forms_expand.T)
    return select * tiled


def local(vertex_start, bare_vertex, bubble, form_mix, cross_tables, freq_perm):
    current = vertex_start[0, 0]
    bare_mat = bare_vertex[0, 0]
    bubble_mat = bubble[0, 0]
    freqs, forms = (bubble_mat.shape[0], bubble_mat.shape[1])
    order_len = current.shape[0]
    momenta = lax.axis_size("mom")
    assert freqs == momenta
    momentum = lax.axis_index("mom")
    channel = lax.axis_index("spin")
    coef_self = jnp.take(jnp.array(COEF_SELF, jnp.float32), channel)
    coef_pair = jnp.take(jnp.array(COEF_PAIR, jnp.float32), channel)

    blocks = current.reshape(freqs, forms, order_len)
    expand = block_rows(order_len, freqs)
    forms_expand = form_rows(order_len, forms)
    packs = []
    mixes = []
    for r in range(2):
        send_order, recv_slots = crossing_plan(cross_tables[r], freq_perm[r], momentum, freqs)
        packs.append(jnp.take(blocks, send_order, axis=0))
        mixes.append(mix_matrix(recv_slots, form_mix[r], freqs, expand, forms_expand))
    stacked = jnp.stack(packs)
    mix = jnp.concatenate(mixes, axis=1)

    bubble_tall = bubble_mat.reshape(order_len, forms)
    block_mask = exact_dot(expand, expand.T)
    bubble_full = exact_dot(bubble_tall, forms_expand.T) * block_mask

    def carry_of(mat):
        return exact_dot(bubble_full, mat)

    carried = carry_of(current)
    bare_part = jnp.dot(bare_mat, carried, preferred_element_type=jnp.float32)

    width = order_len // NCHUNK
    red_chunks = []
    for k in range(NCHUNK):
        cols = slice(k * width, (k + 1) * width)
        received = lax.all_to_all(stacked[..., cols], "mom", split_axis=1, concat_axis=1, tiled=True)
        summed = jnp.dot(
            mix, received.reshape(2 * order_len, width), preferred_element_type=jnp.float32
        ).astype(jnp.bfloat16)
        other = partner_2(summed, "spin", 0)
        red_chunks.append(
            (coef_self * summed.astype(jnp.float32) + coef_pair * other.astype(jnp.float32)).astype(
                jnp.bfloat16
            )
        )
    reducible = jnp.concatenate(red_chunks, axis=1)
    base_sum = bare_mat.astype(jnp.float32) + reducible.astype(jnp.float32)

    total = base_sum + bare_part
    for k in range(NCHUNK):
        rows = slice(k * width, (k + 1) * width)
        total = total + jnp.dot(red_chunks[k], carried[rows], preferred_element_type=jnp.float32)
    current = total.astype(jnp.bfloat16)
    for inner_step in range(1, INNER):
        carried = carry_of(current)
        total = base_sum + jnp.dot(bare_mat, carried, preferred_element_type=jnp.float32)
        total = total + jnp.dot(reducible, carried, preferred_element_type=jnp.float32)
        current = total.astype(jnp.bfloat16)
    return current[None, None]


def solution(mesh):
    in_specs = (
        P("mom", "spin", None, None),
        P("mom", "spin", None, None),
        P("mom", "spin", None, None, None),
        P(),
        P(),
        P(),
    )
    out_specs = P("mom", "spin", None, None)
    return jax.shard_map(local, mesh=mesh, in_specs=in_specs, out_specs=out_specs, check_vma=False)
```

```python
import jax
import jax.numpy as jnp
from jax import lax
from jax.sharding import PartitionSpec as P

INNER = 2
NCHUNK = 2

COEF_SELF = (-0.5, 0.5, 0.5, 0.5)
COEF_PAIR = (-1.5, -0.5, 1.5, -0.5)


def partner_2(value, axis, stride):
    mask = 2**stride
    pairs = [(source, source ^ mask) for source in range(lax.axis_size(axis))]
    return lax.ppermute(value, axis, pairs)


def inverse_perm(perm, size):
    idx = jnp.arange(size, dtype=jnp.int32)
    return jnp.sum(jnp.where(perm[None, :] == idx[:, None], idx[None, :], 0), axis=1)


def crossing_plan(table, frequency_perm, momentum, freqs):
    idx = jnp.arange(freqs, dtype=jnp.int32)
    own_row = jnp.take(table, momentum, axis=0)
    send_order = inverse_perm(own_row, freqs)
    hit = table == momentum
    source = jnp.sum(jnp.where(hit, idx[:, None], 0), axis=0)
    freq_of = inverse_perm(frequency_perm, freqs)
    return send_order, jnp.take(source, freq_of, axis=0)


def block_rows(order_len, freqs):
    forms = order_len // freqs
    rows = lax.broadcasted_iota(jnp.int32, (order_len, freqs), 0) // forms
    cols = lax.broadcasted_iota(jnp.int32, (order_len, freqs), 1)
    return (rows == cols).astype(jnp.bfloat16)


def form_rows(order_len, forms):
    rows = lax.broadcasted_iota(jnp.int32, (order_len, forms), 0) % forms
    cols = lax.broadcasted_iota(jnp.int32, (order_len, forms), 1)
    return (rows == cols).astype(jnp.bfloat16)


def exact_dot(a, b):
    return jnp.dot(a, b, preferred_element_type=jnp.float32).astype(jnp.bfloat16)


def mix_matrix(slots, mixing, freqs, expand, forms_expand):
    idx = jnp.arange(freqs, dtype=jnp.int32)
    onehot = (slots[:, None] == idx[None, :]).astype(jnp.bfloat16)
    select = exact_dot(exact_dot(expand, onehot), expand.T)
    tiled = exact_dot(exact_dot(forms_expand, mixing), forms_expand.T)
    return select * tiled


def local(vertex_start, bare_vertex, bubble, form_mix, cross_tables, freq_perm):
    current = vertex_start[0, 0]
    bare_mat = bare_vertex[0, 0]
    bubble_mat = bubble[0, 0]
    freqs, forms = (bubble_mat.shape[0], bubble_mat.shape[1])
    order_len = current.shape[0]
    momenta = lax.axis_size("mom")
    assert freqs == momenta
    momentum = lax.axis_index("mom")
    channel = lax.axis_index("spin")
    coef_self = jnp.take(jnp.array(COEF_SELF, jnp.float32), channel)
    coef_pair = jnp.take(jnp.array(COEF_PAIR, jnp.float32), channel)

    blocks = current.reshape(freqs, forms, order_len)
    expand = block_rows(order_len, freqs)
    forms_expand = form_rows(order_len, forms)
    packs = []
    mixes = []
    for r in range(2):
        send_order, recv_slots = crossing_plan(cross_tables[r], freq_perm[r], momentum, freqs)
        packs.append(jnp.take(blocks, send_order, axis=0))
        mixes.append(mix_matrix(recv_slots, form_mix[r], freqs, expand, forms_expand))
    stacked = jnp.stack(packs)
    mix = jnp.concatenate(mixes, axis=1)

    bubble_tall = bubble_mat.reshape(order_len, forms)
    block_mask = exact_dot(expand, expand.T)
    bubble_full = exact_dot(bubble_tall, forms_expand.T) * block_mask

    def carry_of(mat):
        return exact_dot(bubble_full, mat)

    carried = carry_of(current)
    bare_part = jnp.dot(bare_mat, carried, preferred_element_type=jnp.float32)

    width = order_len // NCHUNK
    red_chunks = []
    pieces = [stacked[..., k * width:(k + 1) * width] for k in range(NCHUNK)]
    for k in range(NCHUNK):
        received = lax.all_to_all(pieces[k], "mom", split_axis=1, concat_axis=1, tiled=True)
        summed = jnp.dot(
            mix, received.reshape(2 * order_len, width), preferred_element_type=jnp.float32
        ).astype(jnp.bfloat16)
        if k + 1 < NCHUNK:
            summed, pieces[k + 1] = lax.optimization_barrier((summed, pieces[k + 1]))
        other = partner_2(summed, "spin", 0)
        red_chunks.append(
            (coef_self * summed.astype(jnp.float32) + coef_pair * other.astype(jnp.float32)).astype(
                jnp.bfloat16
            )
        )
    reducible = jnp.concatenate(red_chunks, axis=1)
    base_sum = bare_mat.astype(jnp.float32) + reducible.astype(jnp.float32)

    total = base_sum + bare_part
    for k in range(NCHUNK):
        rows = slice(k * width, (k + 1) * width)
        total = total + jnp.dot(red_chunks[k], carried[rows], preferred_element_type=jnp.float32)
    current = total.astype(jnp.bfloat16)
    for inner_step in range(1, INNER):
        carried = carry_of(current)
        total = base_sum + jnp.dot(bare_mat, carried, preferred_element_type=jnp.float32)
        total = total + jnp.dot(reducible, carried, preferred_element_type=jnp.float32)
        current = total.astype(jnp.bfloat16)
    return current[None, None]


def solution(mesh):
    in_specs = (
        P("mom", "spin", None, None),
        P("mom", "spin", None, None),
        P("mom", "spin", None, None, None),
        P(),
        P(),
        P(),
    )
    out_specs = P("mom", "spin", None, None)
    return jax.shard_map(local, mesh=mesh, in_specs=in_specs, out_specs=out_specs, check_vma=False)
```

```python
import jax
import jax.numpy as jnp
from jax import lax
from jax.sharding import PartitionSpec as P

INNER = 2
NCHUNK = 2
NROWS = 2

COEF_SELF = (-0.5, 0.5, 0.5, 0.5)
COEF_PAIR = (-1.5, -0.5, 1.5, -0.5)


def partner_2(value, axis, stride):
    mask = 2**stride
    pairs = [(source, source ^ mask) for source in range(lax.axis_size(axis))]
    return lax.ppermute(value, axis, pairs)


def inverse_perm(perm, size):
    idx = jnp.arange(size, dtype=jnp.int32)
    return jnp.sum(jnp.where(perm[None, :] == idx[:, None], idx[None, :], 0), axis=1)


def crossing_plan(table, frequency_perm, momentum, freqs):
    idx = jnp.arange(freqs, dtype=jnp.int32)
    own_row = jnp.take(table, momentum, axis=0)
    send_order = inverse_perm(own_row, freqs)
    hit = table == momentum
    source = jnp.sum(jnp.where(hit, idx[:, None], 0), axis=0)
    freq_of = inverse_perm(frequency_perm, freqs)
    return send_order, jnp.take(source, freq_of, axis=0)


def block_rows(order_len, freqs):
    forms = order_len // freqs
    rows = lax.broadcasted_iota(jnp.int32, (order_len, freqs), 0) // forms
    cols = lax.broadcasted_iota(jnp.int32, (order_len, freqs), 1)
    return (rows == cols).astype(jnp.bfloat16)


def form_rows(order_len, forms):
    rows = lax.broadcasted_iota(jnp.int32, (order_len, forms), 0) % forms
    cols = lax.broadcasted_iota(jnp.int32, (order_len, forms), 1)
    return (rows == cols).astype(jnp.bfloat16)


def exact_dot(a, b):
    return jnp.dot(a, b, preferred_element_type=jnp.float32).astype(jnp.bfloat16)


def mix_matrix(slots, mixing, freqs, expand, forms_expand):
    idx = jnp.arange(freqs, dtype=jnp.int32)
    onehot = (slots[:, None] == idx[None, :]).astype(jnp.bfloat16)
    select = exact_dot(exact_dot(expand, onehot), expand.T)
    tiled = exact_dot(exact_dot(forms_expand, mixing), forms_expand.T)
    return select * tiled


def local(vertex_start, bare_vertex, bubble, form_mix, cross_tables, freq_perm):
    current = vertex_start[0, 0]
    bare_mat = bare_vertex[0, 0]
    bubble_mat = bubble[0, 0]
    freqs, forms = (bubble_mat.shape[0], bubble_mat.shape[1])
    order_len = current.shape[0]
    momenta = lax.axis_size("mom")
    assert freqs == momenta
    momentum = lax.axis_index("mom")
    channel = lax.axis_index("spin")
    coef_self = jnp.take(jnp.array(COEF_SELF, jnp.float32), channel)
    coef_pair = jnp.take(jnp.array(COEF_PAIR, jnp.float32), channel)

    blocks = current.reshape(freqs, forms, order_len)
    expand = block_rows(order_len, freqs)
    forms_expand = form_rows(order_len, forms)
    packs = []
    mixes = []
    for r in range(2):
        send_order, recv_slots = crossing_plan(cross_tables[r], freq_perm[r], momentum, freqs)
        packs.append(jnp.take(blocks, send_order, axis=0))
        mixes.append(mix_matrix(recv_slots, form_mix[r], freqs, expand, forms_expand))
    stacked = jnp.stack(packs)
    mix = jnp.concatenate(mixes, axis=1)

    bubble_tall = bubble_mat.reshape(order_len, forms)
    block_mask = exact_dot(expand, expand.T)
    bubble_full = exact_dot(bubble_tall, forms_expand.T) * block_mask

    def carry_of(mat):
        return exact_dot(bubble_full, mat)

    carried = carry_of(current)
    bare_part = jnp.dot(bare_mat, carried, preferred_element_type=jnp.float32)

    width = order_len // NCHUNK
    height = order_len // NROWS
    red_chunks = []
    pieces = [stacked[..., k * width:(k + 1) * width] for k in range(NCHUNK)]

    def reduce_pair(summed, other):
        return (coef_self * summed.astype(jnp.float32) + coef_pair * other.astype(jnp.float32)).astype(
            jnp.bfloat16
        )

    early = bare_part
    for k in range(NCHUNK):
        received = lax.all_to_all(pieces[k], "mom", split_axis=1, concat_axis=1, tiled=True)
        summed = jnp.dot(
            mix, received.reshape(2 * order_len, width), preferred_element_type=jnp.float32
        ).astype(jnp.bfloat16)
        if k + 1 < NCHUNK:
            summed, pieces[k + 1] = lax.optimization_barrier((summed, pieces[k + 1]))
            red_chunks.append((summed, partner_2(summed, "spin", 0)))
        else:
            last = [(part, partner_2(part, "spin", 0)) for part in jnp.split(summed, NROWS, axis=0)]
            held = [carried[c * width:(c + 1) * width] for c in range(NCHUNK - 1)]
            sums = [pair[0] for pair in red_chunks]
            summed, held, sums = lax.optimization_barrier((summed, held, sums))
    for c in range(NCHUNK - 1):
        red = reduce_pair(sums[c], red_chunks[c][1])
        red_chunks[c] = red
        early = early + jnp.dot(red, held[c], preferred_element_type=jnp.float32)

    last_carried = carried[(NCHUNK - 1) * width:]
    current_rows = []
    base_rows = []
    red_rows = []
    next_carried = []
    acc = None
    for j in range(NROWS):
        rows = slice(j * height, (j + 1) * height)
        part_sum, part_other = last[j]
        if acc is not None:
            part_other, acc = lax.optimization_barrier((part_other, acc))
        last_red = reduce_pair(part_sum, part_other)
        red_row = jnp.concatenate([c[rows] for c in red_chunks] + [last_red], axis=1)
        base_row = bare_mat[rows].astype(jnp.float32) + red_row.astype(jnp.float32)
        total = base_row + early[rows] + jnp.dot(
            last_red, last_carried, preferred_element_type=jnp.float32
        )
        cur_row = total.astype(jnp.bfloat16)
        carried_row = exact_dot(bubble_full[rows, rows], cur_row)
        part = jnp.dot(bare_mat[:, rows], carried_row, preferred_element_type=jnp.float32)
        acc = part if acc is None else acc + part
        base_rows.append(base_row)
        red_rows.append(red_row)
        next_carried.append(carried_row)
    base_sum = jnp.concatenate(base_rows, axis=0)
    reducible = jnp.concatenate(red_rows, axis=0)
    carried = jnp.concatenate(next_carried, axis=0)
    total = base_sum + acc + jnp.dot(reducible, carried, preferred_element_type=jnp.float32)
    current = total.astype(jnp.bfloat16)
    assert INNER == 2
    return current[None, None]


def solution(mesh):
    in_specs = (
        P("mom", "spin", None, None),
        P("mom", "spin", None, None),
        P("mom", "spin", None, None, None),
        P(),
        P(),
        P(),
    )
    out_specs = P("mom", "spin", None, None)
    return jax.shard_map(local, mesh=mesh, in_specs=in_specs, out_specs=out_specs, check_vma=False)
```

```python
import jax
import jax.numpy as jnp
from jax import lax
from jax.sharding import Mesh, PartitionSpec as P

INNER = 2
NCHUNK = 2

COEF_SELF = (-0.5, 0.5, 0.5, 0.5)
COEF_PAIR = (-1.5, -0.5, 1.5, -0.5)


def partner_2(value, axis, stride):
    mask = 2**stride
    pairs = [(source, source ^ mask) for source in range(lax.axis_size(axis))]
    return lax.ppermute(value, axis, pairs)


def inverse_perm(perm, size):
    idx = jnp.arange(size, dtype=jnp.int32)
    return jnp.sum(jnp.where(perm[None, :] == idx[:, None], idx[None, :], 0), axis=1)


def crossing_plan(table, frequency_perm, momentum, freqs):
    idx = jnp.arange(freqs, dtype=jnp.int32)
    own_row = jnp.take(table, momentum, axis=0)
    send_order = inverse_perm(own_row, freqs)
    hit = table == momentum
    source = jnp.sum(jnp.where(hit, idx[:, None], 0), axis=0)
    freq_of = inverse_perm(frequency_perm, freqs)
    return send_order, jnp.take(source, freq_of, axis=0)


def block_rows(order_len, freqs):
    forms = order_len // freqs
    rows = lax.broadcasted_iota(jnp.int32, (order_len, freqs), 0) // forms
    cols = lax.broadcasted_iota(jnp.int32, (order_len, freqs), 1)
    return (rows == cols).astype(jnp.bfloat16)


def form_rows(order_len, forms):
    rows = lax.broadcasted_iota(jnp.int32, (order_len, forms), 0) % forms
    cols = lax.broadcasted_iota(jnp.int32, (order_len, forms), 1)
    return (rows == cols).astype(jnp.bfloat16)


def exact_dot(a, b):
    return jnp.dot(a, b, preferred_element_type=jnp.float32).astype(jnp.bfloat16)


def mix_matrix(slots, mixing, freqs, expand, forms_expand):
    idx = jnp.arange(freqs, dtype=jnp.int32)
    onehot = (slots[:, None] == idx[None, :]).astype(jnp.bfloat16)
    select = exact_dot(exact_dot(expand, onehot), expand.T)
    tiled = exact_dot(exact_dot(forms_expand, mixing), forms_expand.T)
    return select * tiled


def local(vertex_start, bare_vertex, bubble, form_mix, cross_tables, freq_perm):
    current = vertex_start[0, 0]
    bare_mat = bare_vertex[0, 0]
    bubble_mat = bubble[0, 0]
    freqs, forms = (bubble_mat.shape[0], bubble_mat.shape[1])
    order_len = current.shape[0]
    n_xy = lax.axis_size("xy")
    n_zc = lax.axis_size("zc")
    momenta = n_xy * n_zc
    assert freqs == momenta
    momentum = lax.axis_index("xy") * n_zc + lax.axis_index("zc")
    slot = jnp.arange(momenta, dtype=jnp.int32)
    momentum_of_slot = (slot % n_xy) * n_zc + slot // n_xy
    channel = lax.axis_index("spin")
    coef_self = jnp.take(jnp.array(COEF_SELF, jnp.float32), channel)
    coef_pair = jnp.take(jnp.array(COEF_PAIR, jnp.float32), channel)

    blocks = current.reshape(freqs, forms, order_len)
    expand = block_rows(order_len, freqs)
    forms_expand = form_rows(order_len, forms)
    packs = []
    mixes = []
    for r in range(2):
        send_order, recv_slots = crossing_plan(cross_tables[r], freq_perm[r], momentum, freqs)
        packs.append(jnp.take(blocks, jnp.take(send_order, momentum_of_slot), axis=0))
        recv_at = (recv_slots % n_zc) * n_xy + recv_slots // n_zc
        mixes.append(mix_matrix(recv_at, form_mix[r], freqs, expand, forms_expand))
    stacked = jnp.stack(packs)
    mix = jnp.concatenate(mixes, axis=1)

    bubble_tall = bubble_mat.reshape(order_len, forms)
    block_mask = exact_dot(expand, expand.T)
    bubble_full = exact_dot(bubble_tall, forms_expand.T) * block_mask

    def carry_of(mat):
        return exact_dot(bubble_full, mat)

    carried = carry_of(current)
    bare_part = jnp.dot(bare_mat, carried, preferred_element_type=jnp.float32)

    width = order_len // NCHUNK
    red_chunks = []
    pieces = [stacked[..., k * width:(k + 1) * width] for k in range(NCHUNK)]
    for k in range(NCHUNK):
        staged = pieces[k].reshape(2, n_zc, n_xy, forms, width)
        staged = lax.all_to_all(staged, "zc", split_axis=1, concat_axis=1, tiled=True)
        received = lax.all_to_all(staged, "xy", split_axis=2, concat_axis=2, tiled=True)
        summed = jnp.dot(
            mix, received.reshape(2 * order_len, width), preferred_element_type=jnp.float32
        ).astype(jnp.bfloat16)
        if k + 1 < NCHUNK:
            summed, pieces[k + 1] = lax.optimization_barrier((summed, pieces[k + 1]))
        other = partner_2(summed, "spin", 0)
        red_chunks.append(
            (coef_self * summed.astype(jnp.float32) + coef_pair * other.astype(jnp.float32)).astype(
                jnp.bfloat16
            )
        )
    reducible = jnp.concatenate(red_chunks, axis=1)
    base_sum = bare_mat.astype(jnp.float32) + reducible.astype(jnp.float32)

    total = base_sum + bare_part
    for k in range(NCHUNK):
        rows = slice(k * width, (k + 1) * width)
        total = total + jnp.dot(red_chunks[k], carried[rows], preferred_element_type=jnp.float32)
    current = total.astype(jnp.bfloat16)
    for inner_step in range(1, INNER):
        carried = carry_of(current)
        total = base_sum + jnp.dot(bare_mat, carried, preferred_element_type=jnp.float32)
        total = total + jnp.dot(reducible, carried, preferred_element_type=jnp.float32)
        current = total.astype(jnp.bfloat16)
    return current[None, None]


def solution(mesh):
    momenta, channels = mesh.devices.shape
    n_zc = 4 if momenta % 4 == 0 else 1
    staged_mesh = Mesh(mesh.devices.reshape(momenta // n_zc, n_zc, channels), ("xy", "zc", "spin"))
    vertex = P(("xy", "zc"), "spin", None, None)
    in_specs = (vertex, vertex, P(("xy", "zc"), "spin", None, None, None), P(), P(), P())
    return jax.shard_map(local, mesh=staged_mesh, in_specs=in_specs, out_specs=vertex, check_vma=False)
```

```python
import jax
import jax.numpy as jnp
from jax import lax
from jax.sharding import PartitionSpec as P

INNER = 2
WIDTHS = (256, 512)

COEF_SELF = (-0.5, 0.5, 0.5, 0.5)
COEF_PAIR = (-1.5, -0.5, 1.5, -0.5)


def partner_2(value, axis, stride):
    mask = 2**stride
    pairs = [(source, source ^ mask) for source in range(lax.axis_size(axis))]
    return lax.ppermute(value, axis, pairs)


def inverse_perm(perm, size):
    idx = jnp.arange(size, dtype=jnp.int32)
    return jnp.sum(jnp.where(perm[None, :] == idx[:, None], idx[None, :], 0), axis=1)


def crossing_plan(table, frequency_perm, momentum, freqs):
    idx = jnp.arange(freqs, dtype=jnp.int32)
    own_row = jnp.take(table, momentum, axis=0)
    send_order = inverse_perm(own_row, freqs)
    hit = table == momentum
    source = jnp.sum(jnp.where(hit, idx[:, None], 0), axis=0)
    freq_of = inverse_perm(frequency_perm, freqs)
    return send_order, jnp.take(source, freq_of, axis=0)


def block_rows(order_len, freqs):
    forms = order_len // freqs
    rows = lax.broadcasted_iota(jnp.int32, (order_len, freqs), 0) // forms
    cols = lax.broadcasted_iota(jnp.int32, (order_len, freqs), 1)
    return (rows == cols).astype(jnp.bfloat16)


def form_rows(order_len, forms):
    rows = lax.broadcasted_iota(jnp.int32, (order_len, forms), 0) % forms
    cols = lax.broadcasted_iota(jnp.int32, (order_len, forms), 1)
    return (rows == cols).astype(jnp.bfloat16)


def exact_dot(a, b):
    return jnp.dot(a, b, preferred_element_type=jnp.float32).astype(jnp.bfloat16)


def mix_matrix(slots, mixing, freqs, expand, forms_expand):
    idx = jnp.arange(freqs, dtype=jnp.int32)
    onehot = (slots[:, None] == idx[None, :]).astype(jnp.bfloat16)
    select = exact_dot(exact_dot(expand, onehot), expand.T)
    tiled = exact_dot(exact_dot(forms_expand, mixing), forms_expand.T)
    return select * tiled


def local(vertex_start, bare_vertex, bubble, form_mix, cross_tables, freq_perm):
    current = vertex_start[0, 0]
    bare_mat = bare_vertex[0, 0]
    bubble_mat = bubble[0, 0]
    freqs, forms = (bubble_mat.shape[0], bubble_mat.shape[1])
    order_len = current.shape[0]
    momenta = lax.axis_size("mom")
    assert freqs == momenta
    momentum = lax.axis_index("mom")
    channel = lax.axis_index("spin")
    coef_self = jnp.take(jnp.array(COEF_SELF, jnp.float32), channel)
    coef_pair = jnp.take(jnp.array(COEF_PAIR, jnp.float32), channel)

    blocks = current.reshape(freqs, forms, order_len)
    expand = block_rows(order_len, freqs)
    forms_expand = form_rows(order_len, forms)
    packs = []
    mixes = []
    for r in range(2):
        send_order, recv_slots = crossing_plan(cross_tables[r], freq_perm[r], momentum, freqs)
        packs.append(jnp.take(blocks, send_order, axis=0))
        mixes.append(mix_matrix(recv_slots, form_mix[r], freqs, expand, forms_expand))
    stacked = jnp.stack(packs)
    mix = jnp.concatenate(mixes, axis=1)

    bubble_tall = bubble_mat.reshape(order_len, forms)
    block_mask = exact_dot(expand, expand.T)
    bubble_full = exact_dot(bubble_tall, forms_expand.T) * block_mask

    def carry_of(mat):
        return exact_dot(bubble_full, mat)

    carried = carry_of(current)
    bare_part = jnp.dot(bare_mat, carried, preferred_element_type=jnp.float32)

    assert sum(WIDTHS) == order_len
    starts = [sum(WIDTHS[:k]) for k in range(len(WIDTHS))]
    red_chunks = []
    pieces = [stacked[..., starts[k]:starts[k] + WIDTHS[k]] for k in range(len(WIDTHS))]
    for k in range(len(WIDTHS)):
        received = lax.all_to_all(pieces[k], "mom", split_axis=1, concat_axis=1, tiled=True)
        summed = jnp.dot(
            mix, received.reshape(2 * order_len, WIDTHS[k]), preferred_element_type=jnp.float32
        ).astype(jnp.bfloat16)
        if k + 1 < len(WIDTHS):
            summed, pieces[k + 1] = lax.optimization_barrier((summed, pieces[k + 1]))
        other = partner_2(summed, "spin", 0)
        red_chunks.append(
            (coef_self * summed.astype(jnp.float32) + coef_pair * other.astype(jnp.float32)).astype(
                jnp.bfloat16
            )
        )
    reducible = jnp.concatenate(red_chunks, axis=1)
    base_sum = bare_mat.astype(jnp.float32) + reducible.astype(jnp.float32)

    total = base_sum + bare_part
    for k in range(len(WIDTHS)):
        rows = slice(starts[k], starts[k] + WIDTHS[k])
        total = total + jnp.dot(red_chunks[k], carried[rows], preferred_element_type=jnp.float32)
    current = total.astype(jnp.bfloat16)
    for inner_step in range(1, INNER):
        carried = carry_of(current)
        total = base_sum + jnp.dot(bare_mat, carried, preferred_element_type=jnp.float32)
        total = total + jnp.dot(reducible, carried, preferred_element_type=jnp.float32)
        current = total.astype(jnp.bfloat16)
    return current[None, None]


def solution(mesh):
    in_specs = (
        P("mom", "spin", None, None),
        P("mom", "spin", None, None),
        P("mom", "spin", None, None, None),
        P(),
        P(),
        P(),
    )
    out_specs = P("mom", "spin", None, None)
    return jax.shard_map(local, mesh=mesh, in_specs=in_specs, out_specs=out_specs, check_vma=False)
```

```python
import jax
import jax.numpy as jnp
from jax import lax
from jax.sharding import PartitionSpec as P

INNER = 2
NCHUNK = 2

COEF_SELF = (-0.5, 0.5, 0.5, 0.5)
COEF_PAIR = (-1.5, -0.5, 1.5, -0.5)


def partner_2(value, axis, stride):
    mask = 2**stride
    pairs = [(source, source ^ mask) for source in range(lax.axis_size(axis))]
    return lax.ppermute(value, axis, pairs)


def inverse_perm(perm, size):
    idx = jnp.arange(size, dtype=jnp.int32)
    return jnp.sum(jnp.where(perm[None, :] == idx[:, None], idx[None, :], 0), axis=1)


def crossing_plan(table, frequency_perm, momentum, freqs):
    idx = jnp.arange(freqs, dtype=jnp.int32)
    own_row = jnp.take(table, momentum, axis=0)
    send_order = inverse_perm(own_row, freqs)
    hit = table == momentum
    source = jnp.sum(jnp.where(hit, idx[:, None], 0), axis=0)
    freq_of = inverse_perm(frequency_perm, freqs)
    return send_order, jnp.take(source, freq_of, axis=0)


def block_rows(order_len, freqs):
    forms = order_len // freqs
    rows = lax.broadcasted_iota(jnp.int32, (order_len, freqs), 0) // forms
    cols = lax.broadcasted_iota(jnp.int32, (order_len, freqs), 1)
    return (rows == cols).astype(jnp.bfloat16)


def form_rows(order_len, forms):
    rows = lax.broadcasted_iota(jnp.int32, (order_len, forms), 0) % forms
    cols = lax.broadcasted_iota(jnp.int32, (order_len, forms), 1)
    return (rows == cols).astype(jnp.bfloat16)


def exact_dot(a, b):
    return jnp.dot(a, b, preferred_element_type=jnp.float32).astype(jnp.bfloat16)


def mix_matrix(slots, mixing, freqs, expand, forms_expand):
    idx = jnp.arange(freqs, dtype=jnp.int32)
    onehot = (slots[:, None] == idx[None, :]).astype(jnp.bfloat16)
    select = exact_dot(exact_dot(expand, onehot), expand.T)
    tiled = exact_dot(exact_dot(forms_expand, mixing), forms_expand.T)
    return select * tiled


def local(vertex_start, bare_vertex, bubble, form_mix, cross_tables, freq_perm):
    current = vertex_start[0, 0]
    bare_mat = bare_vertex[0, 0]
    bubble_mat = bubble[0, 0]
    freqs, forms = (bubble_mat.shape[0], bubble_mat.shape[1])
    order_len = current.shape[0]
    momenta = lax.axis_size("mom")
    assert freqs == momenta
    momentum = lax.axis_index("mom")
    channel = lax.axis_index("spin")
    coef_self = sum(jnp.where(channel == c, jnp.float32(v), 0.0) for c, v in enumerate(COEF_SELF))
    coef_pair = sum(jnp.where(channel == c, jnp.float32(v), 0.0) for c, v in enumerate(COEF_PAIR))

    blocks = current.reshape(freqs, forms, order_len)
    expand = block_rows(order_len, freqs)
    forms_expand = form_rows(order_len, forms)
    packs = []
    mixes = []
    for r in range(2):
        send_order, recv_slots = crossing_plan(cross_tables[r], freq_perm[r], momentum, freqs)
        packs.append(jnp.take(blocks, send_order, axis=0))
        mixes.append(mix_matrix(recv_slots, form_mix[r], freqs, expand, forms_expand))
    stacked = jnp.stack(packs)
    mix = jnp.concatenate(mixes, axis=1)

    def carry_of(mat, bubble_mat):
        bubble_tall = bubble_mat.reshape(order_len, forms)
        block_mask = exact_dot(expand, expand.T)
        bubble_full = exact_dot(bubble_tall, forms_expand.T) * block_mask
        return bubble_full, exact_dot(bubble_full, mat)


    width = order_len // NCHUNK
    red_chunks = []
    pieces = [stacked[..., k * width:(k + 1) * width] for k in range(NCHUNK)]
    for k in range(NCHUNK):
        received = lax.all_to_all(pieces[k], "mom", split_axis=1, concat_axis=1, tiled=True)
        summed = jnp.dot(
            mix, received.reshape(2 * order_len, width), preferred_element_type=jnp.float32
        ).astype(jnp.bfloat16)
        if k + 1 == NCHUNK:
            sums = [pair[0] for pair in red_chunks]
            summed, current, bubble_mat, sums = lax.optimization_barrier(
                (summed, current, bubble_mat, sums)
            )
            red_chunks = [(sums[c], red_chunks[c][1]) for c in range(k)]
            bubble_full, carried = carry_of(current, bubble_mat)
            bare_part = jnp.dot(bare_mat, carried, preferred_element_type=jnp.float32)
        if k + 1 < NCHUNK:
            summed, pieces[k + 1] = lax.optimization_barrier((summed, pieces[k + 1]))
        red_chunks.append((summed, partner_2(summed, "spin", 0)))
    red_chunks = [
        (coef_self * summed.astype(jnp.float32) + coef_pair * other.astype(jnp.float32)).astype(
            jnp.bfloat16
        )
        for summed, other in red_chunks
    ]
    reducible = jnp.concatenate(red_chunks, axis=1)
    base_sum = bare_mat.astype(jnp.float32) + reducible.astype(jnp.float32)

    total = base_sum + bare_part
    for k in range(NCHUNK):
        rows = slice(k * width, (k + 1) * width)
        total = total + jnp.dot(red_chunks[k], carried[rows], preferred_element_type=jnp.float32)
    current = total.astype(jnp.bfloat16)
    for inner_step in range(1, INNER):
        carried = exact_dot(bubble_full, current)
        total = base_sum + jnp.dot(bare_mat, carried, preferred_element_type=jnp.float32)
        total = total + jnp.dot(reducible, carried, preferred_element_type=jnp.float32)
        current = total.astype(jnp.bfloat16)
    return current[None, None]


def solution(mesh):
    in_specs = (
        P("mom", "spin", None, None),
        P("mom", "spin", None, None),
        P("mom", "spin", None, None, None),
        P(),
        P(),
        P(),
    )
    out_specs = P("mom", "spin", None, None)
    return jax.shard_map(local, mesh=mesh, in_specs=in_specs, out_specs=out_specs, check_vma=False)
```

```python
import jax
import jax.numpy as jnp
from jax import lax
from jax.sharding import PartitionSpec as P

INNER = 2
NCHUNK = 2

COEF_SELF = (-0.5, 0.5, 0.5, 0.5)
COEF_PAIR = (-1.5, -0.5, 1.5, -0.5)


def partner_2(value, axis, stride):
    mask = 2**stride
    pairs = [(source, source ^ mask) for source in range(lax.axis_size(axis))]
    return lax.ppermute(value, axis, pairs)


def inverse_perm(perm, size):
    idx = jnp.arange(size, dtype=jnp.int32)
    return jnp.sum(jnp.where(perm[None, :] == idx[:, None], idx[None, :], 0), axis=1)


def crossing_plan(table, frequency_perm, momentum, freqs):
    idx = jnp.arange(freqs, dtype=jnp.int32)
    own_row = jnp.take(table, momentum, axis=0)
    send_order = inverse_perm(own_row, freqs)
    hit = table == momentum
    source = jnp.sum(jnp.where(hit, idx[:, None], 0), axis=0)
    freq_of = inverse_perm(frequency_perm, freqs)
    return send_order, jnp.take(source, freq_of, axis=0)


def block_rows(order_len, freqs):
    forms = order_len // freqs
    rows = lax.broadcasted_iota(jnp.int32, (order_len, freqs), 0) // forms
    cols = lax.broadcasted_iota(jnp.int32, (order_len, freqs), 1)
    return (rows == cols).astype(jnp.bfloat16)


def form_rows(order_len, forms):
    rows = lax.broadcasted_iota(jnp.int32, (order_len, forms), 0) % forms
    cols = lax.broadcasted_iota(jnp.int32, (order_len, forms), 1)
    return (rows == cols).astype(jnp.bfloat16)


def exact_dot(a, b):
    return jnp.dot(a, b, preferred_element_type=jnp.float32).astype(jnp.bfloat16)


def mix_matrix(slots, mixing, freqs, expand, forms_expand):
    idx = jnp.arange(freqs, dtype=jnp.int32)
    onehot = (slots[:, None] == idx[None, :]).astype(jnp.bfloat16)
    select = exact_dot(exact_dot(expand, onehot), expand.T)
    tiled = exact_dot(exact_dot(forms_expand, mixing), forms_expand.T)
    return select * tiled


def local(vertex_start, bare_vertex, bubble, form_mix, cross_tables, freq_perm):
    current = vertex_start[0, 0]
    bare_mat = bare_vertex[0, 0]
    bubble_mat = bubble[0, 0]
    freqs, forms = (bubble_mat.shape[0], bubble_mat.shape[1])
    order_len = current.shape[0]
    momenta = lax.axis_size("mom")
    assert freqs == momenta
    momentum = lax.axis_index("mom")
    channel = lax.axis_index("spin")
    coef_self = jnp.take(jnp.array(COEF_SELF, jnp.float32), channel)
    coef_pair = jnp.take(jnp.array(COEF_PAIR, jnp.float32), channel)

    expand = block_rows(order_len, freqs)
    forms_expand = form_rows(order_len, forms)
    same_form = exact_dot(forms_expand, forms_expand.T)
    idx = jnp.arange(freqs, dtype=jnp.int32)
    selects = []
    mixes = []
    for r in range(2):
        send_order, recv_slots = crossing_plan(cross_tables[r], freq_perm[r], momentum, freqs)
        onehot = (send_order[:, None] == idx[None, :]).astype(jnp.bfloat16)
        selects.append(exact_dot(exact_dot(expand, onehot), expand.T) * same_form)
        mixes.append(mix_matrix(recv_slots, form_mix[r], freqs, expand, forms_expand))
    select = jnp.concatenate(selects, axis=0)
    mix = jnp.concatenate(mixes, axis=1)

    bubble_tall = bubble_mat.reshape(order_len, forms)
    block_mask = exact_dot(expand, expand.T)
    bubble_full = exact_dot(bubble_tall, forms_expand.T) * block_mask

    def carry_of(mat):
        return exact_dot(bubble_full, mat)

    carried = carry_of(current)
    bare_part = jnp.dot(bare_mat, carried, preferred_element_type=jnp.float32)

    width = order_len // NCHUNK
    red_chunks = []
    pieces = [
        exact_dot(select, current[:, k * width:(k + 1) * width]).reshape(2, freqs, forms, width)
        for k in range(NCHUNK)
    ]
    for k in range(NCHUNK):
        received = lax.all_to_all(pieces[k], "mom", split_axis=1, concat_axis=1, tiled=True)
        summed = jnp.dot(
            mix, received.reshape(2 * order_len, width), preferred_element_type=jnp.float32
        ).astype(jnp.bfloat16)
        if k + 1 < NCHUNK:
            summed, pieces[k + 1] = lax.optimization_barrier((summed, pieces[k + 1]))
        other = partner_2(summed, "spin", 0)
        red_chunks.append(
            (coef_self * summed.astype(jnp.float32) + coef_pair * other.astype(jnp.float32)).astype(
                jnp.bfloat16
            )
        )
    reducible = jnp.concatenate(red_chunks, axis=1)
    base_sum = bare_mat.astype(jnp.float32) + reducible.astype(jnp.float32)

    total = base_sum + bare_part
    for k in range(NCHUNK):
        rows = slice(k * width, (k + 1) * width)
        total = total + jnp.dot(red_chunks[k], carried[rows], preferred_element_type=jnp.float32)
    current = total.astype(jnp.bfloat16)
    for inner_step in range(1, INNER):
        carried = carry_of(current)
        total = base_sum + jnp.dot(bare_mat, carried, preferred_element_type=jnp.float32)
        total = total + jnp.dot(reducible, carried, preferred_element_type=jnp.float32)
        current = total.astype(jnp.bfloat16)
    return current[None, None]


def solution(mesh):
    in_specs = (
        P("mom", "spin", None, None),
        P("mom", "spin", None, None),
        P("mom", "spin", None, None, None),
        P(),
        P(),
        P(),
    )
    out_specs = P("mom", "spin", None, None)
    return jax.shard_map(local, mesh=mesh, in_specs=in_specs, out_specs=out_specs, check_vma=False)
```

```python
import jax
import jax.numpy as jnp
from jax import lax
from jax.sharding import PartitionSpec as P

INNER = 2
NCHUNK = 2

COEF_SELF = (-0.5, 0.5, 0.5, 0.5)
COEF_PAIR = (-1.5, -0.5, 1.5, -0.5)


def partner_2(value, axis, stride):
    mask = 2**stride
    pairs = [(source, source ^ mask) for source in range(lax.axis_size(axis))]
    return lax.ppermute(value, axis, pairs)


def inverse_perm(perm, size):
    idx = jnp.arange(size, dtype=jnp.int32)
    return jnp.sum(jnp.where(perm[None, :] == idx[:, None], idx[None, :], 0), axis=1)


def crossing_plan(table, frequency_perm, momentum, freqs):
    idx = jnp.arange(freqs, dtype=jnp.int32)
    own_row = jnp.take(table, momentum, axis=0)
    send_order = inverse_perm(own_row, freqs)
    hit = table == momentum
    source = jnp.sum(jnp.where(hit, idx[:, None], 0), axis=0)
    freq_of = inverse_perm(frequency_perm, freqs)
    return send_order, jnp.take(source, freq_of, axis=0)


def block_rows(order_len, freqs):
    forms = order_len // freqs
    rows = lax.broadcasted_iota(jnp.int32, (order_len, freqs), 0) // forms
    cols = lax.broadcasted_iota(jnp.int32, (order_len, freqs), 1)
    return (rows == cols).astype(jnp.bfloat16)


def form_rows(order_len, forms):
    rows = lax.broadcasted_iota(jnp.int32, (order_len, forms), 0) % forms
    cols = lax.broadcasted_iota(jnp.int32, (order_len, forms), 1)
    return (rows == cols).astype(jnp.bfloat16)


def exact_dot(a, b):
    return jnp.dot(a, b, preferred_element_type=jnp.float32).astype(jnp.bfloat16)


def mix_matrix(slots, mixing, freqs, expand, forms_expand):
    idx = jnp.arange(freqs, dtype=jnp.int32)
    onehot = (slots[:, None] == idx[None, :]).astype(jnp.bfloat16)
    select = exact_dot(exact_dot(expand, onehot), expand.T)
    tiled = exact_dot(exact_dot(forms_expand, mixing), forms_expand.T)
    return select * tiled


def local(vertex_start, bare_vertex, bubble, form_mix, cross_tables, freq_perm):
    current = vertex_start[0, 0]
    bare_mat = bare_vertex[0, 0]
    bubble_mat = bubble[0, 0]
    freqs, forms = (bubble_mat.shape[0], bubble_mat.shape[1])
    order_len = current.shape[0]
    momenta = lax.axis_size("mom")
    assert freqs == momenta
    momentum = lax.axis_index("mom")
    channel = lax.axis_index("spin")
    coef_self = jnp.take(jnp.array(COEF_SELF, jnp.float32), channel)
    coef_pair = jnp.take(jnp.array(COEF_PAIR, jnp.float32), channel)

    blocks = current.reshape(freqs, forms, order_len)
    expand = block_rows(order_len, freqs)
    forms_expand = form_rows(order_len, forms)
    packs = []
    mixes = []
    for r in range(2):
        send_order, recv_slots = crossing_plan(cross_tables[r], freq_perm[r], momentum, freqs)
        packs.append(jnp.take(blocks, send_order, axis=0))
        mixes.append(mix_matrix(recv_slots, form_mix[r], freqs, expand, forms_expand))
    stacked = jnp.stack(packs)
    mix4 = jnp.concatenate(mixes, axis=1).reshape(order_len, 2, freqs, forms)

    bubble_tall = bubble_mat.reshape(order_len, forms)
    block_mask = exact_dot(expand, expand.T)
    bubble_full = exact_dot(bubble_tall, forms_expand.T) * block_mask

    def carry_of(mat):
        return exact_dot(bubble_full, mat)

    carried = carry_of(current)
    bare_part = jnp.dot(bare_mat, carried, preferred_element_type=jnp.float32)

    width = order_len // NCHUNK
    red_chunks = []
    pieces = [stacked[..., k * width:(k + 1) * width] for k in range(NCHUNK)]
    for k in range(NCHUNK):
        received = lax.all_to_all(pieces[k], "mom", split_axis=1, concat_axis=1, tiled=True)
        summed = jnp.einsum(
            "frqm,rqmb->fb", mix4, received, preferred_element_type=jnp.float32
        ).astype(jnp.bfloat16)
        if k + 1 < NCHUNK:
            summed, pieces[k + 1] = lax.optimization_barrier((summed, pieces[k + 1]))
        other = partner_2(summed, "spin", 0)
        red_chunks.append(
            (coef_self * summed.astype(jnp.float32) + coef_pair * other.astype(jnp.float32)).astype(
                jnp.bfloat16
            )
        )
    reducible = jnp.concatenate(red_chunks, axis=1)
    base_sum = bare_mat.astype(jnp.float32) + reducible.astype(jnp.float32)

    total = base_sum + bare_part
    for k in range(NCHUNK):
        rows = slice(k * width, (k + 1) * width)
        total = total + jnp.dot(red_chunks[k], carried[rows], preferred_element_type=jnp.float32)
    current = total.astype(jnp.bfloat16)
    for inner_step in range(1, INNER):
        carried = carry_of(current)
        total = base_sum + jnp.dot(bare_mat, carried, preferred_element_type=jnp.float32)
        total = total + jnp.dot(reducible, carried, preferred_element_type=jnp.float32)
        current = total.astype(jnp.bfloat16)
    return current[None, None]


def solution(mesh):
    in_specs = (
        P("mom", "spin", None, None),
        P("mom", "spin", None, None),
        P("mom", "spin", None, None, None),
        P(),
        P(),
        P(),
    )
    out_specs = P("mom", "spin", None, None)
    return jax.shard_map(local, mesh=mesh, in_specs=in_specs, out_specs=out_specs, check_vma=False)
```

```python
import jax
import jax.numpy as jnp
from jax import lax
from jax.sharding import PartitionSpec as P

INNER = 2
WIDTHS = (512, 256)
NCHUNK = len(WIDTHS)

COEF_SELF = (-0.5, 0.5, 0.5, 0.5)
COEF_PAIR = (-1.5, -0.5, 1.5, -0.5)


def partner_2(value, axis, stride):
    mask = 2**stride
    pairs = [(source, source ^ mask) for source in range(lax.axis_size(axis))]
    return lax.ppermute(value, axis, pairs)


def inverse_perm(perm, size):
    idx = jnp.arange(size, dtype=jnp.int32)
    return jnp.sum(jnp.where(perm[None, :] == idx[:, None], idx[None, :], 0), axis=1)


def crossing_plan(table, frequency_perm, momentum, freqs):
    idx = jnp.arange(freqs, dtype=jnp.int32)
    own_row = jnp.take(table, momentum, axis=0)
    send_order = inverse_perm(own_row, freqs)
    hit = table == momentum
    source = jnp.sum(jnp.where(hit, idx[:, None], 0), axis=0)
    freq_of = inverse_perm(frequency_perm, freqs)
    return send_order, jnp.take(source, freq_of, axis=0)


def block_rows(order_len, freqs):
    forms = order_len // freqs
    rows = lax.broadcasted_iota(jnp.int32, (order_len, freqs), 0) // forms
    cols = lax.broadcasted_iota(jnp.int32, (order_len, freqs), 1)
    return (rows == cols).astype(jnp.bfloat16)


def form_rows(order_len, forms):
    rows = lax.broadcasted_iota(jnp.int32, (order_len, forms), 0) % forms
    cols = lax.broadcasted_iota(jnp.int32, (order_len, forms), 1)
    return (rows == cols).astype(jnp.bfloat16)


def exact_dot(a, b):
    return jnp.dot(a, b, preferred_element_type=jnp.float32).astype(jnp.bfloat16)


def mix_matrix(slots, mixing, freqs, expand, forms_expand):
    idx = jnp.arange(freqs, dtype=jnp.int32)
    onehot = (slots[:, None] == idx[None, :]).astype(jnp.bfloat16)
    select = exact_dot(exact_dot(expand, onehot), expand.T)
    tiled = exact_dot(exact_dot(forms_expand, mixing), forms_expand.T)
    return select * tiled


def local(vertex_start, bare_vertex, bubble, form_mix, cross_tables, freq_perm):
    current = vertex_start[0, 0]
    bare_mat = bare_vertex[0, 0]
    bubble_mat = bubble[0, 0]
    freqs, forms = (bubble_mat.shape[0], bubble_mat.shape[1])
    order_len = current.shape[0]
    momenta = lax.axis_size("mom")
    assert freqs == momenta
    momentum = lax.axis_index("mom")
    channel = lax.axis_index("spin")
    coef_self = sum(jnp.where(channel == c, jnp.float32(v), 0.0) for c, v in enumerate(COEF_SELF))
    coef_pair = sum(jnp.where(channel == c, jnp.float32(v), 0.0) for c, v in enumerate(COEF_PAIR))

    blocks = current.reshape(freqs, forms, order_len)
    expand = block_rows(order_len, freqs)
    forms_expand = form_rows(order_len, forms)
    packs = []
    mixes = []
    for r in range(2):
        send_order, recv_slots = crossing_plan(cross_tables[r], freq_perm[r], momentum, freqs)
        packs.append(jnp.take(blocks, send_order, axis=0))
        mixes.append(mix_matrix(recv_slots, form_mix[r], freqs, expand, forms_expand))
    stacked = jnp.stack(packs)
    mix = jnp.concatenate(mixes, axis=1)

    def carry_of(mat, bubble_mat):
        bubble_tall = bubble_mat.reshape(order_len, forms)
        block_mask = exact_dot(expand, expand.T)
        bubble_full = exact_dot(bubble_tall, forms_expand.T) * block_mask
        return bubble_full, exact_dot(bubble_full, mat)


    assert sum(WIDTHS) == order_len
    starts = [sum(WIDTHS[:k]) for k in range(NCHUNK)]
    red_chunks = []
    pieces = [stacked[..., starts[k]:starts[k] + WIDTHS[k]] for k in range(NCHUNK)]
    for k in range(NCHUNK):
        received = lax.all_to_all(pieces[k], "mom", split_axis=1, concat_axis=1, tiled=True)
        summed = jnp.dot(
            mix, received.reshape(2 * order_len, WIDTHS[k]), preferred_element_type=jnp.float32
        ).astype(jnp.bfloat16)
        if k + 1 == NCHUNK:
            sums = [pair[0] for pair in red_chunks]
            summed, current, bubble_mat, sums = lax.optimization_barrier(
                (summed, current, bubble_mat, sums)
            )
            red_chunks = [(sums[c], red_chunks[c][1]) for c in range(k)]
            bubble_full, carried = carry_of(current, bubble_mat)
            bare_part = jnp.dot(bare_mat, carried, preferred_element_type=jnp.float32)
        if k + 1 < NCHUNK:
            summed, pieces[k + 1] = lax.optimization_barrier((summed, pieces[k + 1]))
        red_chunks.append((summed, partner_2(summed, "spin", 0)))
    red_chunks = [
        (coef_self * summed.astype(jnp.float32) + coef_pair * other.astype(jnp.float32)).astype(
            jnp.bfloat16
        )
        for summed, other in red_chunks
    ]
    reducible = jnp.concatenate(red_chunks, axis=1)
    base_sum = bare_mat.astype(jnp.float32) + reducible.astype(jnp.float32)

    total = base_sum + bare_part
    for k in range(NCHUNK):
        rows = slice(starts[k], starts[k] + WIDTHS[k])
        total = total + jnp.dot(red_chunks[k], carried[rows], preferred_element_type=jnp.float32)
    current = total.astype(jnp.bfloat16)
    for inner_step in range(1, INNER):
        carried = exact_dot(bubble_full, current)
        total = base_sum + jnp.dot(bare_mat, carried, preferred_element_type=jnp.float32)
        total = total + jnp.dot(reducible, carried, preferred_element_type=jnp.float32)
        current = total.astype(jnp.bfloat16)
    return current[None, None]


def solution(mesh):
    in_specs = (
        P("mom", "spin", None, None),
        P("mom", "spin", None, None),
        P("mom", "spin", None, None, None),
        P(),
        P(),
        P(),
    )
    out_specs = P("mom", "spin", None, None)
    return jax.shard_map(local, mesh=mesh, in_specs=in_specs, out_specs=out_specs, check_vma=False)
```

```python
import jax
import jax.numpy as jnp
from jax import lax
from jax.sharding import PartitionSpec as P

INNER = 2
WIDTHS = (512, 256)
NCHUNK = len(WIDTHS)

COEF_SELF = (-0.5, 0.5, 0.5, 0.5)
COEF_PAIR = (-1.5, -0.5, 1.5, -0.5)


def partner_2(value, axis, stride):
    mask = 2**stride
    pairs = [(source, source ^ mask) for source in range(lax.axis_size(axis))]
    return lax.ppermute(value, axis, pairs)


def inverse_perm(perm, size):
    idx = jnp.arange(size, dtype=jnp.int32)
    return jnp.sum(jnp.where(perm[None, :] == idx[:, None], idx[None, :], 0), axis=1)


def crossing_plan(table, frequency_perm, momentum, freqs):
    idx = jnp.arange(freqs, dtype=jnp.int32)
    own_row = jnp.take(table, momentum, axis=0)
    send_order = inverse_perm(own_row, freqs)
    hit = table == momentum
    source = jnp.sum(jnp.where(hit, idx[:, None], 0), axis=0)
    freq_of = inverse_perm(frequency_perm, freqs)
    return send_order, jnp.take(source, freq_of, axis=0)


def block_rows(order_len, freqs):
    forms = order_len // freqs
    rows = lax.broadcasted_iota(jnp.int32, (order_len, freqs), 0) // forms
    cols = lax.broadcasted_iota(jnp.int32, (order_len, freqs), 1)
    return (rows == cols).astype(jnp.bfloat16)


def form_rows(order_len, forms):
    rows = lax.broadcasted_iota(jnp.int32, (order_len, forms), 0) % forms
    cols = lax.broadcasted_iota(jnp.int32, (order_len, forms), 1)
    return (rows == cols).astype(jnp.bfloat16)


def exact_dot(a, b):
    return jnp.dot(a, b, preferred_element_type=jnp.float32).astype(jnp.bfloat16)


def mix_matrix(slots, mixing, freqs, expand, forms_expand):
    idx = jnp.arange(freqs, dtype=jnp.int32)
    onehot = (slots[:, None] == idx[None, :]).astype(jnp.bfloat16)
    select = exact_dot(exact_dot(expand, onehot), expand.T)
    tiled = exact_dot(exact_dot(forms_expand, mixing), forms_expand.T)
    return select * tiled


def local(vertex_start, bare_vertex, bubble, form_mix, cross_tables, freq_perm):
    current = vertex_start[0, 0]
    bare_mat = bare_vertex[0, 0]
    bubble_mat = bubble[0, 0]
    freqs, forms = (bubble_mat.shape[0], bubble_mat.shape[1])
    order_len = current.shape[0]
    momenta = lax.axis_size("mom")
    assert freqs == momenta
    momentum = lax.axis_index("mom")
    channel = lax.axis_index("spin")
    coef_self = sum(jnp.where(channel == c, jnp.float32(v), 0.0) for c, v in enumerate(COEF_SELF))
    coef_pair = sum(jnp.where(channel == c, jnp.float32(v), 0.0) for c, v in enumerate(COEF_PAIR))

    expand = block_rows(order_len, freqs)
    forms_expand = form_rows(order_len, forms)
    packs = []
    mixes = []
    for r in range(2):
        send_order, recv_slots = crossing_plan(cross_tables[r], freq_perm[r], momentum, freqs)
        packs.append(send_order)
        mixes.append(mix_matrix(recv_slots, form_mix[r], freqs, expand, forms_expand))
    mix = jnp.concatenate(mixes, axis=1)

    def carry_of(mat, bubble_mat):
        bubble_tall = bubble_mat.reshape(order_len, forms)
        block_mask = exact_dot(expand, expand.T)
        bubble_full = exact_dot(bubble_tall, forms_expand.T) * block_mask
        return bubble_full, exact_dot(bubble_full, mat)


    assert sum(WIDTHS) == order_len
    starts = [sum(WIDTHS[:k]) for k in range(NCHUNK)]
    red_chunks = []
    pieces = []
    for k in range(NCHUNK):
        blocks = current[:, starts[k]:starts[k] + WIDTHS[k]].reshape(freqs, forms, WIDTHS[k])
        pieces.append(jnp.stack([jnp.take(blocks, order, axis=0) for order in packs]))
    for k in range(NCHUNK):
        received = lax.all_to_all(pieces[k], "mom", split_axis=1, concat_axis=1, tiled=True)
        summed = jnp.dot(
            mix, received.reshape(2 * order_len, WIDTHS[k]), preferred_element_type=jnp.float32
        ).astype(jnp.bfloat16)
        if k + 1 == NCHUNK:
            sums = [pair[0] for pair in red_chunks]
            summed, current, bubble_mat, sums = lax.optimization_barrier(
                (summed, current, bubble_mat, sums)
            )
            red_chunks = [(sums[c], red_chunks[c][1]) for c in range(k)]
            bubble_full, carried = carry_of(current, bubble_mat)
            bare_part = jnp.dot(bare_mat, carried, preferred_element_type=jnp.float32)
        if k + 1 < NCHUNK:
            summed, pieces[k + 1] = lax.optimization_barrier((summed, pieces[k + 1]))
        red_chunks.append((summed, partner_2(summed, "spin", 0)))
    red_chunks = [
        (coef_self * summed.astype(jnp.float32) + coef_pair * other.astype(jnp.float32)).astype(
            jnp.bfloat16
        )
        for summed, other in red_chunks
    ]
    reducible = jnp.concatenate(red_chunks, axis=1)
    base_sum = bare_mat.astype(jnp.float32) + reducible.astype(jnp.float32)

    total = base_sum + bare_part
    for k in range(NCHUNK):
        rows = slice(starts[k], starts[k] + WIDTHS[k])
        total = total + jnp.dot(red_chunks[k], carried[rows], preferred_element_type=jnp.float32)
    current = total.astype(jnp.bfloat16)
    for inner_step in range(1, INNER):
        carried = exact_dot(bubble_full, current)
        total = base_sum + jnp.dot(bare_mat, carried, preferred_element_type=jnp.float32)
        total = total + jnp.dot(reducible, carried, preferred_element_type=jnp.float32)
        current = total.astype(jnp.bfloat16)
    return current[None, None]


def solution(mesh):
    in_specs = (
        P("mom", "spin", None, None),
        P("mom", "spin", None, None),
        P("mom", "spin", None, None, None),
        P(),
        P(),
        P(),
    )
    out_specs = P("mom", "spin", None, None)
    return jax.shard_map(local, mesh=mesh, in_specs=in_specs, out_specs=out_specs, check_vma=False)
```

```python
import jax
import jax.numpy as jnp
from jax import lax
from jax.sharding import PartitionSpec as P

INNER = 2
WIDTHS = (512, 256)
NCHUNK = len(WIDTHS)

COEF_SELF = (-0.5, 0.5, 0.5, 0.5)
COEF_PAIR = (-1.5, -0.5, 1.5, -0.5)


def partner_2(value, axis, stride):
    mask = 2**stride
    pairs = [(source, source ^ mask) for source in range(lax.axis_size(axis))]
    return lax.ppermute(value, axis, pairs)


def inverse_perm(perm, size):
    idx = jnp.arange(size, dtype=jnp.int32)
    return jnp.sum(jnp.where(perm[None, :] == idx[:, None], idx[None, :], 0), axis=1)


def crossing_plan(table, frequency_perm, momentum, freqs):
    idx = jnp.arange(freqs, dtype=jnp.int32)
    own_row = jnp.take(table, momentum, axis=0)
    send_order = inverse_perm(own_row, freqs)
    hit = table == momentum
    source = jnp.sum(jnp.where(hit, idx[:, None], 0), axis=0)
    freq_of = inverse_perm(frequency_perm, freqs)
    return send_order, jnp.take(source, freq_of, axis=0)


def block_rows(order_len, freqs):
    forms = order_len // freqs
    rows = lax.broadcasted_iota(jnp.int32, (order_len, freqs), 0) // forms
    cols = lax.broadcasted_iota(jnp.int32, (order_len, freqs), 1)
    return (rows == cols).astype(jnp.bfloat16)


def form_rows(order_len, forms):
    rows = lax.broadcasted_iota(jnp.int32, (order_len, forms), 0) % forms
    cols = lax.broadcasted_iota(jnp.int32, (order_len, forms), 1)
    return (rows == cols).astype(jnp.bfloat16)


def exact_dot(a, b):
    return jnp.dot(a, b, preferred_element_type=jnp.float32).astype(jnp.bfloat16)


def mix_matrix(slots, mixing, freqs, expand, forms_expand):
    idx = jnp.arange(freqs, dtype=jnp.int32)
    onehot = (slots[:, None] == idx[None, :]).astype(jnp.bfloat16)
    select = exact_dot(exact_dot(expand, onehot), expand.T)
    tiled = exact_dot(exact_dot(forms_expand, mixing), forms_expand.T)
    return select * tiled


def local(vertex_start, bare_vertex, bubble, form_mix, cross_tables, freq_perm):
    current = vertex_start[0, 0]
    bare_mat = bare_vertex[0, 0]
    bubble_mat = bubble[0, 0]
    freqs, forms = (bubble_mat.shape[0], bubble_mat.shape[1])
    order_len = current.shape[0]
    momenta = lax.axis_size("mom")
    assert freqs == momenta
    momentum = lax.axis_index("mom")
    channel = lax.axis_index("spin")
    coef_self = sum(jnp.where(channel == c, jnp.float32(v), 0.0) for c, v in enumerate(COEF_SELF))
    coef_pair = sum(jnp.where(channel == c, jnp.float32(v), 0.0) for c, v in enumerate(COEF_PAIR))

    expand = block_rows(order_len, freqs)
    forms_expand = form_rows(order_len, forms)
    packs = []
    mixes = []
    for r in range(2):
        send_order, recv_slots = crossing_plan(cross_tables[r], freq_perm[r], momentum, freqs)
        packs.append(send_order)
        mixes.append(mix_matrix(recv_slots, form_mix[r], freqs, expand, forms_expand))
    mix = jnp.concatenate(mixes, axis=1)

    def carry_of(mat, bubble_mat):
        bubble_tall = bubble_mat.reshape(order_len, forms)
        block_mask = exact_dot(expand, expand.T)
        bubble_full = exact_dot(bubble_tall, forms_expand.T) * block_mask
        return bubble_full, exact_dot(bubble_full, mat)


    assert sum(WIDTHS) == order_len
    starts = [sum(WIDTHS[:k]) for k in range(NCHUNK)]
    red_chunks = []
    pieces = []
    for k in range(NCHUNK):
        blocks = current[:, starts[k]:starts[k] + WIDTHS[k]].reshape(freqs, forms, WIDTHS[k])
        pieces.append(jnp.stack([jnp.take(blocks, order, axis=0) for order in packs]))
    for k in range(NCHUNK):
        received = lax.all_to_all(pieces[k], "mom", split_axis=1, concat_axis=1, tiled=True)
        summed = jnp.dot(
            mix, received.reshape(2 * order_len, WIDTHS[k]), preferred_element_type=jnp.float32
        ).astype(jnp.bfloat16)
        if k + 1 == NCHUNK:
            sums = [pair[0] for pair in red_chunks]
            summed, current, bubble_mat, sums = lax.optimization_barrier(
                (summed, current, bubble_mat, sums)
            )
            red_chunks = [(sums[c], red_chunks[c][1]) for c in range(k)]
            bubble_full, carried = carry_of(current, bubble_mat)
            bare_part = jnp.dot(bare_mat, carried, preferred_element_type=jnp.float32)
        if k + 1 < NCHUNK:
            summed, pieces[k + 1] = lax.optimization_barrier((summed, pieces[k + 1]))
        red_chunks.append((summed, partner_2(summed, "spin", 0)))
    reduce_pair = lambda summed, other: (
        coef_self * summed.astype(jnp.float32) + coef_pair * other.astype(jnp.float32)
    ).astype(jnp.bfloat16)
    red_chunks = [reduce_pair(*pair) for pair in red_chunks[:-1]] + [red_chunks[-1]]
    early = bare_part
    for k in range(NCHUNK - 1):
        rows = slice(starts[k], starts[k] + WIDTHS[k])
        early = early + jnp.dot(red_chunks[k], carried[rows], preferred_element_type=jnp.float32)
    last_sum, last_other = red_chunks[-1]
    last_other, early = lax.optimization_barrier((last_other, early))
    red_chunks[-1] = reduce_pair(last_sum, last_other)
    reducible = jnp.concatenate(red_chunks, axis=1)
    base_sum = bare_mat.astype(jnp.float32) + reducible.astype(jnp.float32)

    rows = slice(starts[-1], order_len)
    total = base_sum + early + jnp.dot(red_chunks[-1], carried[rows], preferred_element_type=jnp.float32)
    current = total.astype(jnp.bfloat16)
    for inner_step in range(1, INNER):
        carried = exact_dot(bubble_full, current)
        total = base_sum + jnp.dot(bare_mat, carried, preferred_element_type=jnp.float32)
        total = total + jnp.dot(reducible, carried, preferred_element_type=jnp.float32)
        current = total.astype(jnp.bfloat16)
    return current[None, None]


def solution(mesh):
    in_specs = (
        P("mom", "spin", None, None),
        P("mom", "spin", None, None),
        P("mom", "spin", None, None, None),
        P(),
        P(),
        P(),
    )
    out_specs = P("mom", "spin", None, None)
    return jax.shard_map(local, mesh=mesh, in_specs=in_specs, out_specs=out_specs, check_vma=False)
```

```python
import jax
import jax.numpy as jnp
from jax import lax
from jax.sharding import PartitionSpec as P

INNER = 2
WIDTHS = (512, 256)
NCHUNK = len(WIDTHS)
TILE = 192

COEF_SELF = (-0.5, 0.5, 0.5, 0.5)
COEF_PAIR = (-1.5, -0.5, 1.5, -0.5)


def partner_2(value, axis, stride):
    mask = 2**stride
    pairs = [(source, source ^ mask) for source in range(lax.axis_size(axis))]
    return lax.ppermute(value, axis, pairs)


def inverse_perm(perm, size):
    idx = jnp.arange(size, dtype=jnp.int32)
    return jnp.sum(jnp.where(perm[None, :] == idx[:, None], idx[None, :], 0), axis=1)


def crossing_plan(table, frequency_perm, momentum, freqs):
    idx = jnp.arange(freqs, dtype=jnp.int32)
    own_row = jnp.take(table, momentum, axis=0)
    send_order = inverse_perm(own_row, freqs)
    hit = table == momentum
    source = jnp.sum(jnp.where(hit, idx[:, None], 0), axis=0)
    freq_of = inverse_perm(frequency_perm, freqs)
    return send_order, jnp.take(source, freq_of, axis=0)


def block_rows(order_len, freqs):
    forms = order_len // freqs
    rows = lax.broadcasted_iota(jnp.int32, (order_len, freqs), 0) // forms
    cols = lax.broadcasted_iota(jnp.int32, (order_len, freqs), 1)
    return (rows == cols).astype(jnp.bfloat16)


def form_rows(order_len, forms):
    rows = lax.broadcasted_iota(jnp.int32, (order_len, forms), 0) % forms
    cols = lax.broadcasted_iota(jnp.int32, (order_len, forms), 1)
    return (rows == cols).astype(jnp.bfloat16)


def exact_dot(a, b):
    return jnp.dot(a, b, preferred_element_type=jnp.float32).astype(jnp.bfloat16)


def mix_matrix(slots, mixing, freqs, expand, forms_expand):
    idx = jnp.arange(freqs, dtype=jnp.int32)
    onehot = (slots[:, None] == idx[None, :]).astype(jnp.bfloat16)
    select = exact_dot(exact_dot(expand, onehot), expand.T)
    tiled = exact_dot(exact_dot(forms_expand, mixing), forms_expand.T)
    return select * tiled


def local(vertex_start, bare_vertex, bubble, form_mix, cross_tables, freq_perm):
    current = vertex_start[0, 0]
    bare_mat = bare_vertex[0, 0]
    bubble_mat = bubble[0, 0]
    freqs, forms = (bubble_mat.shape[0], bubble_mat.shape[1])
    order_len = current.shape[0]
    momenta = lax.axis_size("mom")
    assert freqs == momenta
    momentum = lax.axis_index("mom")
    channel = lax.axis_index("spin")
    coef_self = sum(jnp.where(channel == c, jnp.float32(v), 0.0) for c, v in enumerate(COEF_SELF))
    coef_pair = sum(jnp.where(channel == c, jnp.float32(v), 0.0) for c, v in enumerate(COEF_PAIR))

    expand = block_rows(order_len, freqs)
    forms_expand = form_rows(order_len, forms)
    packs = []
    mixes = []
    for r in range(2):
        send_order, recv_slots = crossing_plan(cross_tables[r], freq_perm[r], momentum, freqs)
        packs.append(send_order)
        mixes.append(mix_matrix(recv_slots, form_mix[r], freqs, expand, forms_expand))
    mix = jnp.concatenate(mixes, axis=1)

    def carry_of(mat, bubble_mat):
        bubble_tall = bubble_mat.reshape(order_len, forms)
        block_mask = exact_dot(expand, expand.T)
        bubble_full = exact_dot(bubble_tall, forms_expand.T) * block_mask
        return bubble_full, diagonal_dot(bubble_full, mat)

    def diagonal_dot(full, mat):
        tile = TILE if order_len % TILE == 0 and TILE % forms == 0 else order_len
        parts = [
            exact_dot(full[i:i + tile, i:i + tile], mat[i:i + tile]) for i in range(0, order_len, tile)
        ]
        return jnp.concatenate(parts, axis=0)


    assert sum(WIDTHS) == order_len
    starts = [sum(WIDTHS[:k]) for k in range(NCHUNK)]
    red_chunks = []
    pieces = []
    for k in range(NCHUNK):
        blocks = current[:, starts[k]:starts[k] + WIDTHS[k]].reshape(freqs, forms, WIDTHS[k])
        pieces.append(jnp.stack([jnp.take(blocks, order, axis=0) for order in packs]))
    for k in range(NCHUNK):
        received = lax.all_to_all(pieces[k], "mom", split_axis=1, concat_axis=1, tiled=True)
        summed = jnp.dot(
            mix, received.reshape(2 * order_len, WIDTHS[k]), preferred_element_type=jnp.float32
        ).astype(jnp.bfloat16)
        if k + 1 == NCHUNK:
            sums = [pair[0] for pair in red_chunks]
            summed, current, bubble_mat, sums = lax.optimization_barrier(
                (summed, current, bubble_mat, sums)
            )
            red_chunks = [(sums[c], red_chunks[c][1]) for c in range(k)]
            bubble_full, carried = carry_of(current, bubble_mat)
            bare_part = jnp.dot(bare_mat, carried, preferred_element_type=jnp.float32)
        if k + 1 < NCHUNK:
            summed, pieces[k + 1] = lax.optimization_barrier((summed, pieces[k + 1]))
        red_chunks.append((summed, partner_2(summed, "spin", 0)))
    reduce_pair = lambda summed, other: (
        coef_self * summed.astype(jnp.float32) + coef_pair * other.astype(jnp.float32)
    ).astype(jnp.bfloat16)
    red_chunks = [reduce_pair(*pair) for pair in red_chunks[:-1]] + [red_chunks[-1]]
    early = bare_part
    for k in range(NCHUNK - 1):
        rows = slice(starts[k], starts[k] + WIDTHS[k])
        early = early + jnp.dot(red_chunks[k], carried[rows], preferred_element_type=jnp.float32)
    last_sum, last_other = red_chunks[-1]
    last_other, early = lax.optimization_barrier((last_other, early))
    red_chunks[-1] = reduce_pair(last_sum, last_other)
    reducible = jnp.concatenate(red_chunks, axis=1)
    base_sum = bare_mat.astype(jnp.float32) + reducible.astype(jnp.float32)

    rows = slice(starts[-1], order_len)
    total = base_sum + early + jnp.dot(red_chunks[-1], carried[rows], preferred_element_type=jnp.float32)
    current = total.astype(jnp.bfloat16)
    for inner_step in range(1, INNER):
        carried = diagonal_dot(bubble_full, current)
        total = base_sum + jnp.dot(bare_mat, carried, preferred_element_type=jnp.float32)
        total = total + jnp.dot(reducible, carried, preferred_element_type=jnp.float32)
        current = total.astype(jnp.bfloat16)
    return current[None, None]


def solution(mesh):
    in_specs = (
        P("mom", "spin", None, None),
        P("mom", "spin", None, None),
        P("mom", "spin", None, None, None),
        P(),
        P(),
        P(),
    )
    out_specs = P("mom", "spin", None, None)
    return jax.shard_map(local, mesh=mesh, in_specs=in_specs, out_specs=out_specs, check_vma=False)
```

```python
import jax
import jax.numpy as jnp
from jax import lax
from jax.sharding import PartitionSpec as P

INNER = 2
WIDTHS = (512, 256)
NCHUNK = len(WIDTHS)
TILE = 192

COEF_SELF = (-0.5, 0.5, 0.5, 0.5)
COEF_PAIR = (-1.5, -0.5, 1.5, -0.5)


def partner_2(value, axis, stride):
    mask = 2**stride
    pairs = [(source, source ^ mask) for source in range(lax.axis_size(axis))]
    return lax.ppermute(value, axis, pairs)


def inverse_perm(perm, size):
    idx = jnp.arange(size, dtype=jnp.int32)
    return jnp.sum(jnp.where(perm[None, :] == idx[:, None], idx[None, :], 0), axis=1)


def crossing_plan(table, frequency_perm, momentum, freqs):
    idx = jnp.arange(freqs, dtype=jnp.int32)
    own_row = jnp.take(table, momentum, axis=0)
    send_order = inverse_perm(own_row, freqs)
    hit = table == momentum
    source = jnp.sum(jnp.where(hit, idx[:, None], 0), axis=0)
    freq_of = inverse_perm(frequency_perm, freqs)
    return send_order, jnp.take(source, freq_of, axis=0)


def block_rows(order_len, freqs):
    forms = order_len // freqs
    rows = lax.broadcasted_iota(jnp.int32, (order_len, freqs), 0) // forms
    cols = lax.broadcasted_iota(jnp.int32, (order_len, freqs), 1)
    return (rows == cols).astype(jnp.bfloat16)


def form_rows(order_len, forms):
    rows = lax.broadcasted_iota(jnp.int32, (order_len, forms), 0) % forms
    cols = lax.broadcasted_iota(jnp.int32, (order_len, forms), 1)
    return (rows == cols).astype(jnp.bfloat16)


def exact_dot(a, b):
    return jnp.dot(a, b, preferred_element_type=jnp.float32).astype(jnp.bfloat16)


def mix_matrix(slots, mixing, freqs, expand, forms_expand):
    idx = jnp.arange(freqs, dtype=jnp.int32)
    onehot = (slots[:, None] == idx[None, :]).astype(jnp.bfloat16)
    select = exact_dot(exact_dot(expand, onehot), expand.T)
    tiled = exact_dot(exact_dot(forms_expand, mixing), forms_expand.T)
    return select * tiled


def local(vertex_start, bare_vertex, bubble, form_mix, cross_tables, freq_perm):
    current = vertex_start[0, 0]
    bare_mat = bare_vertex[0, 0]
    bubble_mat = bubble[0, 0]
    freqs, forms = (bubble_mat.shape[0], bubble_mat.shape[1])
    order_len = current.shape[0]
    momenta = lax.axis_size("mom")
    assert freqs == momenta
    momentum = lax.axis_index("mom")
    channel = lax.axis_index("spin")
    coef_self = sum(jnp.where(channel == c, jnp.float32(v), 0.0) for c, v in enumerate(COEF_SELF))
    coef_pair = sum(jnp.where(channel == c, jnp.float32(v), 0.0) for c, v in enumerate(COEF_PAIR))

    expand = block_rows(order_len, freqs)
    forms_expand = form_rows(order_len, forms)
    packs = []
    mixes = []
    for r in range(2):
        send_order, recv_slots = crossing_plan(cross_tables[r], freq_perm[r], momentum, freqs)
        packs.append(send_order)
        mixes.append(mix_matrix(recv_slots, form_mix[r], freqs, expand, forms_expand))
    mix4 = jnp.concatenate(mixes, axis=1).reshape(order_len, 2, freqs, forms)

    def carry_of(mat, bubble_mat):
        bubble_tall = bubble_mat.reshape(order_len, forms)
        block_mask = exact_dot(expand, expand.T)
        bubble_full = exact_dot(bubble_tall, forms_expand.T) * block_mask
        return bubble_full, diagonal_dot(bubble_full, mat)

    def diagonal_dot(full, mat):
        tile = TILE if order_len % TILE == 0 and TILE % forms == 0 else order_len
        parts = [
            exact_dot(full[i:i + tile, i:i + tile], mat[i:i + tile]) for i in range(0, order_len, tile)
        ]
        return jnp.concatenate(parts, axis=0)


    assert sum(WIDTHS) == order_len
    starts = [sum(WIDTHS[:k]) for k in range(NCHUNK)]
    red_chunks = []
    pieces = []
    for k in range(NCHUNK):
        blocks = current[:, starts[k]:starts[k] + WIDTHS[k]].reshape(freqs, forms, WIDTHS[k])
        pieces.append(jnp.stack([jnp.take(blocks, order, axis=0) for order in packs]))
    for k in range(NCHUNK):
        received = lax.all_to_all(pieces[k], "mom", split_axis=1, concat_axis=1, tiled=True)
        summed = jnp.einsum(
            "frqm,rqmb->fb", mix4, received, preferred_element_type=jnp.float32
        ).astype(jnp.bfloat16)
        if k + 1 == NCHUNK:
            sums = [pair[0] for pair in red_chunks]
            summed, current, bubble_mat, sums = lax.optimization_barrier(
                (summed, current, bubble_mat, sums)
            )
            red_chunks = [(sums[c], red_chunks[c][1]) for c in range(k)]
            bubble_full, carried = carry_of(current, bubble_mat)
            bare_part = jnp.dot(bare_mat, carried, preferred_element_type=jnp.float32)
        if k + 1 < NCHUNK:
            summed, pieces[k + 1] = lax.optimization_barrier((summed, pieces[k + 1]))
        red_chunks.append((summed, partner_2(summed, "spin", 0)))
    reduce_pair = lambda summed, other: (
        coef_self * summed.astype(jnp.float32) + coef_pair * other.astype(jnp.float32)
    ).astype(jnp.bfloat16)
    red_chunks = [reduce_pair(*pair) for pair in red_chunks[:-1]] + [red_chunks[-1]]
    early = bare_part
    for k in range(NCHUNK - 1):
        rows = slice(starts[k], starts[k] + WIDTHS[k])
        early = early + jnp.dot(red_chunks[k], carried[rows], preferred_element_type=jnp.float32)
    last_sum, last_other = red_chunks[-1]
    last_other, early = lax.optimization_barrier((last_other, early))
    red_chunks[-1] = reduce_pair(last_sum, last_other)
    reducible = jnp.concatenate(red_chunks, axis=1)
    base_sum = bare_mat.astype(jnp.float32) + reducible.astype(jnp.float32)

    rows = slice(starts[-1], order_len)
    total = base_sum + early + jnp.dot(red_chunks[-1], carried[rows], preferred_element_type=jnp.float32)
    current = total.astype(jnp.bfloat16)
    for inner_step in range(1, INNER):
        carried = diagonal_dot(bubble_full, current)
        total = base_sum + jnp.dot(bare_mat, carried, preferred_element_type=jnp.float32)
        total = total + jnp.dot(reducible, carried, preferred_element_type=jnp.float32)
        current = total.astype(jnp.bfloat16)
    return current[None, None]


def solution(mesh):
    in_specs = (
        P("mom", "spin", None, None),
        P("mom", "spin", None, None),
        P("mom", "spin", None, None, None),
        P(),
        P(),
        P(),
    )
    out_specs = P("mom", "spin", None, None)
    return jax.shard_map(local, mesh=mesh, in_specs=in_specs, out_specs=out_specs, check_vma=False)
```

```python
import jax
import jax.numpy as jnp
from jax import lax
from jax.sharding import PartitionSpec as P

INNER = 2
WIDTHS = (512, 256)
NCHUNK = len(WIDTHS)
TILE = 96

COEF_SELF = (-0.5, 0.5, 0.5, 0.5)
COEF_PAIR = (-1.5, -0.5, 1.5, -0.5)


def partner_2(value, axis, stride):
    mask = 2**stride
    pairs = [(source, source ^ mask) for source in range(lax.axis_size(axis))]
    return lax.ppermute(value, axis, pairs)


def inverse_perm(perm, size):
    idx = jnp.arange(size, dtype=jnp.int32)
    return jnp.sum(jnp.where(perm[None, :] == idx[:, None], idx[None, :], 0), axis=1)


def crossing_plan(table, frequency_perm, momentum, freqs):
    idx = jnp.arange(freqs, dtype=jnp.int32)
    own_row = jnp.take(table, momentum, axis=0)
    send_order = inverse_perm(own_row, freqs)
    hit = table == momentum
    source = jnp.sum(jnp.where(hit, idx[:, None], 0), axis=0)
    freq_of = inverse_perm(frequency_perm, freqs)
    return send_order, jnp.take(source, freq_of, axis=0)


def block_rows(order_len, freqs):
    forms = order_len // freqs
    rows = lax.broadcasted_iota(jnp.int32, (order_len, freqs), 0) // forms
    cols = lax.broadcasted_iota(jnp.int32, (order_len, freqs), 1)
    return (rows == cols).astype(jnp.bfloat16)


def form_rows(order_len, forms):
    rows = lax.broadcasted_iota(jnp.int32, (order_len, forms), 0) % forms
    cols = lax.broadcasted_iota(jnp.int32, (order_len, forms), 1)
    return (rows == cols).astype(jnp.bfloat16)


def exact_dot(a, b):
    return jnp.dot(a, b, preferred_element_type=jnp.float32).astype(jnp.bfloat16)


def mix_matrix(slots, mixing, freqs, expand, forms_expand):
    idx = jnp.arange(freqs, dtype=jnp.int32)
    onehot = (slots[:, None] == idx[None, :]).astype(jnp.bfloat16)
    select = exact_dot(exact_dot(expand, onehot), expand.T)
    tiled = exact_dot(exact_dot(forms_expand, mixing), forms_expand.T)
    return select * tiled


def local(vertex_start, bare_vertex, bubble, form_mix, cross_tables, freq_perm):
    current = vertex_start[0, 0]
    bare_mat = bare_vertex[0, 0]
    bubble_mat = bubble[0, 0]
    freqs, forms = (bubble_mat.shape[0], bubble_mat.shape[1])
    order_len = current.shape[0]
    momenta = lax.axis_size("mom")
    assert freqs == momenta
    momentum = lax.axis_index("mom")
    channel = lax.axis_index("spin")
    coef_self = sum(jnp.where(channel == c, jnp.float32(v), 0.0) for c, v in enumerate(COEF_SELF))
    coef_pair = sum(jnp.where(channel == c, jnp.float32(v), 0.0) for c, v in enumerate(COEF_PAIR))

    expand = block_rows(order_len, freqs)
    forms_expand = form_rows(order_len, forms)
    packs = []
    mixes = []
    for r in range(2):
        send_order, recv_slots = crossing_plan(cross_tables[r], freq_perm[r], momentum, freqs)
        packs.append(send_order)
        mixes.append(mix_matrix(recv_slots, form_mix[r], freqs, expand, forms_expand))
    mix4 = jnp.concatenate(mixes, axis=1).reshape(order_len, 2, freqs, forms)

    def carry_of(mat, bubble_mat):
        bubble_tall = bubble_mat.reshape(order_len, forms)
        block_mask = exact_dot(expand, expand.T)
        bubble_full = exact_dot(bubble_tall, forms_expand.T) * block_mask
        return bubble_full, diagonal_dot(bubble_full, mat)

    def diagonal_dot(full, mat):
        tile = TILE if order_len % TILE == 0 and TILE % forms == 0 else order_len
        parts = [
            exact_dot(full[i:i + tile, i:i + tile], mat[i:i + tile]) for i in range(0, order_len, tile)
        ]
        return jnp.concatenate(parts, axis=0)


    assert sum(WIDTHS) == order_len
    starts = [sum(WIDTHS[:k]) for k in range(NCHUNK)]
    red_chunks = []
    pieces = []
    for k in range(NCHUNK):
        blocks = current[:, starts[k]:starts[k] + WIDTHS[k]].reshape(freqs, forms, WIDTHS[k])
        pieces.append(jnp.stack([jnp.take(blocks, order, axis=0) for order in packs]))
    for k in range(NCHUNK):
        received = lax.all_to_all(pieces[k], "mom", split_axis=1, concat_axis=1, tiled=True)
        summed = jnp.einsum(
            "frqm,rqmb->fb", mix4, received, preferred_element_type=jnp.float32
        ).astype(jnp.bfloat16)
        if k + 1 == NCHUNK:
            sums = [pair[0] for pair in red_chunks]
            summed, current, bubble_mat, sums = lax.optimization_barrier(
                (summed, current, bubble_mat, sums)
            )
            red_chunks = [(sums[c], red_chunks[c][1]) for c in range(k)]
            bubble_full, carried = carry_of(current, bubble_mat)
            bare_part = jnp.dot(bare_mat, carried, preferred_element_type=jnp.float32)
        if k + 1 < NCHUNK:
            summed, pieces[k + 1] = lax.optimization_barrier((summed, pieces[k + 1]))
        red_chunks.append((summed, partner_2(summed, "spin", 0)))
    reduce_pair = lambda summed, other: (
        coef_self * summed.astype(jnp.float32) + coef_pair * other.astype(jnp.float32)
    ).astype(jnp.bfloat16)
    red_chunks = [reduce_pair(*pair) for pair in red_chunks[:-1]] + [red_chunks[-1]]
    early = bare_part
    for k in range(NCHUNK - 1):
        rows = slice(starts[k], starts[k] + WIDTHS[k])
        early = early + jnp.dot(red_chunks[k], carried[rows], preferred_element_type=jnp.float32)
    last_sum, last_other = red_chunks[-1]
    last_other, early = lax.optimization_barrier((last_other, early))
    red_chunks[-1] = reduce_pair(last_sum, last_other)
    reducible = jnp.concatenate(red_chunks, axis=1)
    base_sum = bare_mat.astype(jnp.float32) + reducible.astype(jnp.float32)

    rows = slice(starts[-1], order_len)
    total = base_sum + early + jnp.dot(red_chunks[-1], carried[rows], preferred_element_type=jnp.float32)
    current = total.astype(jnp.bfloat16)
    pair_left = jnp.concatenate([bare_mat, reducible], axis=1)
    for inner_step in range(1, INNER):
        carried = diagonal_dot(bubble_full, current)
        total = base_sum + jnp.dot(
            pair_left, jnp.concatenate([carried, carried], axis=0), preferred_element_type=jnp.float32
        )
        current = total.astype(jnp.bfloat16)
    return current[None, None]


def solution(mesh):
    in_specs = (
        P("mom", "spin", None, None),
        P("mom", "spin", None, None),
        P("mom", "spin", None, None, None),
        P(),
        P(),
        P(),
    )
    out_specs = P("mom", "spin", None, None)
    return jax.shard_map(local, mesh=mesh, in_specs=in_specs, out_specs=out_specs, check_vma=False)
```

```python
import jax
import jax.numpy as jnp
from jax import lax
from jax.sharding import PartitionSpec as P

INNER = 2
WIDTHS = (512, 256)
NCHUNK = len(WIDTHS)
TILE = 48

COEF_SELF = (-0.5, 0.5, 0.5, 0.5)
COEF_PAIR = (-1.5, -0.5, 1.5, -0.5)


def partner_2(value, axis, stride):
    mask = 2**stride
    pairs = [(source, source ^ mask) for source in range(lax.axis_size(axis))]
    return lax.ppermute(value, axis, pairs)


def inverse_perm(perm, size):
    idx = jnp.arange(size, dtype=jnp.int32)
    return jnp.sum(jnp.where(perm[None, :] == idx[:, None], idx[None, :], 0), axis=1)


def crossing_plan(table, frequency_perm, momentum, freqs):
    idx = jnp.arange(freqs, dtype=jnp.int32)
    own_row = jnp.take(table, momentum, axis=0)
    send_order = inverse_perm(own_row, freqs)
    hit = table == momentum
    source = jnp.sum(jnp.where(hit, idx[:, None], 0), axis=0)
    freq_of = inverse_perm(frequency_perm, freqs)
    return send_order, jnp.take(source, freq_of, axis=0)


def block_rows(order_len, freqs):
    forms = order_len // freqs
    rows = lax.broadcasted_iota(jnp.int32, (order_len, freqs), 0) // forms
    cols = lax.broadcasted_iota(jnp.int32, (order_len, freqs), 1)
    return (rows == cols).astype(jnp.bfloat16)


def form_rows(order_len, forms):
    rows = lax.broadcasted_iota(jnp.int32, (order_len, forms), 0) % forms
    cols = lax.broadcasted_iota(jnp.int32, (order_len, forms), 1)
    return (rows == cols).astype(jnp.bfloat16)


def exact_dot(a, b):
    return jnp.dot(a, b, preferred_element_type=jnp.float32).astype(jnp.bfloat16)


def mix_matrix(slots, mixing, freqs, expand, forms_expand):
    idx = jnp.arange(freqs, dtype=jnp.int32)
    onehot = (slots[:, None] == idx[None, :]).astype(jnp.bfloat16)
    select = exact_dot(exact_dot(expand, onehot), expand.T)
    tiled = exact_dot(exact_dot(forms_expand, mixing), forms_expand.T)
    return select * tiled


def local(vertex_start, bare_vertex, bubble, form_mix, cross_tables, freq_perm):
    current = vertex_start[0, 0]
    bare_mat = bare_vertex[0, 0]
    bubble_mat = bubble[0, 0]
    freqs, forms = (bubble_mat.shape[0], bubble_mat.shape[1])
    order_len = current.shape[0]
    momenta = lax.axis_size("mom")
    assert freqs == momenta
    momentum = lax.axis_index("mom")
    channel = lax.axis_index("spin")
    coef_self = sum(jnp.where(channel == c, jnp.float32(v), 0.0) for c, v in enumerate(COEF_SELF))
    coef_pair = sum(jnp.where(channel == c, jnp.float32(v), 0.0) for c, v in enumerate(COEF_PAIR))

    expand = block_rows(order_len, freqs)
    forms_expand = form_rows(order_len, forms)
    packs = []
    mixes = []
    for r in range(2):
        send_order, recv_slots = crossing_plan(cross_tables[r], freq_perm[r], momentum, freqs)
        packs.append(send_order)
        mixes.append(mix_matrix(recv_slots, form_mix[r], freqs, expand, forms_expand))
    mix4 = jnp.concatenate(mixes, axis=1).reshape(order_len, 2, freqs, forms)

    def carry_of(mat, bubble_mat):
        bubble_tall = bubble_mat.reshape(order_len, forms)
        block_mask = exact_dot(expand, expand.T)
        bubble_full = exact_dot(bubble_tall, forms_expand.T) * block_mask
        return bubble_full, diagonal_dot(bubble_full, mat)

    def diagonal_dot(full, mat):
        tile = TILE if order_len % TILE == 0 and TILE % forms == 0 else order_len
        parts = [
            exact_dot(full[i:i + tile, i:i + tile], mat[i:i + tile]) for i in range(0, order_len, tile)
        ]
        return jnp.concatenate(parts, axis=0)


    assert sum(WIDTHS) == order_len
    starts = [sum(WIDTHS[:k]) for k in range(NCHUNK)]
    red_chunks = []
    pieces = []
    for k in range(NCHUNK):
        blocks = current[:, starts[k]:starts[k] + WIDTHS[k]].reshape(freqs, forms, WIDTHS[k])
        pieces.append(jnp.stack([jnp.take(blocks, order, axis=0) for order in packs]))
    for k in range(NCHUNK):
        received = lax.all_to_all(pieces[k], "mom", split_axis=1, concat_axis=1, tiled=True)
        summed = jnp.einsum(
            "frqm,rqmb->fb", mix4, received, preferred_element_type=jnp.float32
        ).astype(jnp.bfloat16)
        if k + 1 == NCHUNK:
            sums = [pair[0] for pair in red_chunks]
            summed, current, bubble_mat, sums = lax.optimization_barrier(
                (summed, current, bubble_mat, sums)
            )
            red_chunks = [(sums[c], red_chunks[c][1]) for c in range(k)]
            bubble_full, carried = carry_of(current, bubble_mat)
            bare_part = jnp.dot(bare_mat, carried, preferred_element_type=jnp.float32)
        if k + 1 < NCHUNK:
            summed, pieces[k + 1] = lax.optimization_barrier((summed, pieces[k + 1]))
        red_chunks.append((summed, partner_2(summed, "spin", 0)))
    reduce_pair = lambda summed, other: (
        coef_self * summed.astype(jnp.float32) + coef_pair * other.astype(jnp.float32)
    ).astype(jnp.bfloat16)
    red_chunks = [reduce_pair(*pair) for pair in red_chunks[:-1]] + [red_chunks[-1]]
    early = bare_part
    for k in range(NCHUNK - 1):
        rows = slice(starts[k], starts[k] + WIDTHS[k])
        early = early + jnp.dot(red_chunks[k], carried[rows], preferred_element_type=jnp.float32)
    last_sum, last_other = red_chunks[-1]
    last_other, early = lax.optimization_barrier((last_other, early))
    red_chunks[-1] = reduce_pair(last_sum, last_other)
    reducible = jnp.concatenate(red_chunks, axis=1)
    base_sum = bare_mat.astype(jnp.float32) + reducible.astype(jnp.float32)

    rows = slice(starts[-1], order_len)
    total = base_sum + early + jnp.dot(red_chunks[-1], carried[rows], preferred_element_type=jnp.float32)
    current = total.astype(jnp.bfloat16)
    pair_left = jnp.concatenate([bare_mat, reducible], axis=1)
    for inner_step in range(1, INNER):
        carried = diagonal_dot(bubble_full, current)
        total = base_sum + jnp.dot(
            pair_left, jnp.concatenate([carried, carried], axis=0), preferred_element_type=jnp.float32
        )
        current = total.astype(jnp.bfloat16)
    return current[None, None]


def solution(mesh):
    in_specs = (
        P("mom", "spin", None, None),
        P("mom", "spin", None, None),
        P("mom", "spin", None, None, None),
        P(),
        P(),
        P(),
    )
    out_specs = P("mom", "spin", None, None)
    return jax.shard_map(local, mesh=mesh, in_specs=in_specs, out_specs=out_specs, check_vma=False)
```
